256 devices in a mesh: patch: 8 (over z_hi, core), seq: 16 (over y, x), cfg: 2 (over z_lo).
Axes of the slice: x: 4, y: 4, z: 8 (z_hi: 4, z_lo: 2; z = z_hi * 2 + z_lo), core: 2. Of those that a mesh axis runs over, the one named last changes fastest.
Arguments:
- query: bfloat16 [36864, 2048], P(('cfg', 'patch', 'seq')), parts along dimension 0, may hold values from -16 to 16
- fresh_key: bfloat16 [36864, 2048], P(('cfg', 'patch', 'seq')), parts along dimension 0, may hold values from -6 to 6
- fresh_value: bfloat16 [36864, 2048], P(('cfg', 'patch', 'seq')), parts along dimension 0, may hold values from -6 to 6
- stale_key: bfloat16 [36864, 2048], P(('cfg', 'patch', 'seq')), parts along dimension 0, may hold values from -6 to 6
- stale_value: bfloat16 [36864, 2048], P(('cfg', 'patch', 'seq')), parts along dimension 0, may hold values from -6 to 6
- key_tiles: int32 [48, 18], P('patch'), may hold values from 0 to 47, as said below
- tile_count: int32 [48], P('patch'), may hold values from 1 to 18
Outputs:
- attended: bfloat16 [36864, 2048], P(('cfg', 'patch', 'seq')), parts along dimension 0
The draws below stay inside these ranges and needn't reach their ends.
There are 2 independent parts, one for each index of `cfg`. The reference program is written for one: setup_inputs(seed, part) draws one part's arguments, and reference() takes and returns one part's arrays. A program takes and returns all parts, laid end to end along the dimension named above; an argument that names none is the same for every part. Nothing has to cross between parts.
Inputs may be any that keep to these rules, and one draw needn't show every extreme that they name: `key_tiles`: tile numbers are patch * 2 * 3 + row * 3 + column. The first tile_count[t] entries of row t are distinct tiles within one tile of t in patch, row and column (t itself among them); the other entries equal t and are ignored.
All inputs are finite; a program needn't handle non-finite values.
Results may differ from the reference program's by a relative error of at most 0.0049.
Values may be sent and summed in bfloat16 or wider, within the bound.
No kernel may reach another device: no remote copies, remote signals or barrier semaphores. Data moves between devices by JAX's collectives and lax.ppermute only.
A program may use at most 64 MiB of HBM per device.

```python
import jax
import jax.numpy as jnp
import numpy as np
from jax import lax

NUM_HEADS = 16
HEAD_DIM = 128
TILE_TOKENS = 384
TILES_H = 2
TILES_W = 3
KEY_SLOTS = 18
TOKENS = 18432
ALL_TILES = 48


neighbour_table = np.array([[a, b, c] for a in (-1, 0, 1) for b in (-1, 0, 1) for c in (-1, 0, 1)], dtype=np.int32)


def tile_lists(key):
    per_patch = TILES_H * TILES_W
    patches = ALL_TILES // per_patch
    tiles = jnp.arange(ALL_TILES, dtype=jnp.int32)
    patch_of = tiles // per_patch
    rest = tiles % per_patch
    row_of = rest // TILES_W
    col_of = rest % TILES_W
    offsets = jnp.asarray(neighbour_table)
    near_patch = patch_of[:, None] + offsets[None, :, 0]
    near_row = row_of[:, None] + offsets[None, :, 1]
    near_col = col_of[:, None] + offsets[None, :, 2]
    inside = (near_patch >= 0) & (near_patch < patches) & (near_row >= 0) & (near_row < TILES_H) & (near_col >= 0) & (near_col < TILES_W)
    candidate = near_patch * per_patch + near_row * TILES_W + near_col
    coins = jax.random.randint(jax.random.fold_in(key, 11), (ALL_TILES, 27), 0, 4) > 0
    center = (offsets[:, 0] == 0) & (offsets[:, 1] == 0) & (offsets[:, 2] == 0)
    forced_tile = per_patch + min(1, TILES_H - 1) * TILES_W + min(1, TILES_W - 1)
    keep = inside & (coins | center[None, :] | (tiles == forced_tile)[:, None])
    noise = jax.random.randint(jax.random.fold_in(key, 12), (ALL_TILES, 27), 0, 65536)
    score = jnp.where(keep, 0, 1 << 22) + noise * 32 + jnp.arange(27, dtype=jnp.int32)[None, :]
    order = jnp.argsort(score, axis=1)[:, :KEY_SLOTS]
    picked = jnp.take_along_axis(candidate, order, axis=1)
    count = jnp.sum(keep.astype(jnp.int32), axis=1).astype(jnp.int32)
    slot = jnp.arange(KEY_SLOTS, dtype=jnp.int32)
    listed = jnp.where(slot[None, :] < count[:, None], picked, tiles[:, None])
    return (listed.astype(jnp.int32), count)


def draw_key_tiles(key, part):
    return tile_lists(key)[0]


def draw_tile_count(key, part):
    return tile_lists(key)[1]


def steps_of(stream_key, dims, split, smallest, largest):
    def one(dim, shards_of):
        draws = jax.random.uniform(jax.random.fold_in(jax.random.fold_in(stream_key, 6), dim), (shards_of,), jnp.float32, smallest / len(split), largest / len(split))
        return jnp.repeat(jnp.exp(draws), dims[dim] // shards_of).reshape((-1,) + (1,) * (len(dims) - dim - 1))

    level = one(*split[0])
    for cut in split[1:]:
        level = level * one(*cut)
    return level


def gaussian(own_key, extent, deviation, most, pieces=(), kind=jnp.bfloat16):
    entries = deviation * jax.random.normal(own_key, extent, jnp.float32)
    if pieces:
        entries = entries * steps_of(own_key, extent, pieces, -0.22, 0.18)
    return jnp.clip(entries, -most, most).astype(kind)


def setup_inputs(seed: int = 0, part: int = 0) -> dict:
    arg_keys = jax.random.split(jax.random.key(seed), 8)
    part_splits = jax.random.split(jax.random.fold_in(arg_keys[7], part), 8)
    return {
        "query": gaussian(part_splits[0], (TOKENS, NUM_HEADS * HEAD_DIM), 4.0, 16.0, ((0, 128),)),
        "fresh_key": gaussian(part_splits[1], (TOKENS, NUM_HEADS * HEAD_DIM), 1.0, 6.0, ((0, 128),)),
        "fresh_value": gaussian(part_splits[2], (TOKENS, NUM_HEADS * HEAD_DIM), 1.0, 6.0, ((0, 128),)),
        "stale_key": gaussian(part_splits[3], (TOKENS, NUM_HEADS * HEAD_DIM), 1.0, 6.0, ((0, 128),)),
        "stale_value": gaussian(part_splits[4], (TOKENS, NUM_HEADS * HEAD_DIM), 1.0, 6.0, ((0, 128),)),
        "key_tiles": draw_key_tiles(jax.random.fold_in(arg_keys[7], 71), part),
        "tile_count": draw_tile_count(jax.random.fold_in(arg_keys[7], 71), part),
    }


soft_cap = 8.0


def reference(query, fresh_key, fresh_value, stale_key, stale_value, key_tiles, tile_count):
    per_patch = TILES_H * TILES_W
    scale = 1.0 / (HEAD_DIM ** 0.5)

    def as_tiles(array):
        return array.reshape(ALL_TILES, TILE_TOKENS, NUM_HEADS, HEAD_DIM)

    query_t = as_tiles(query)
    fresh_k = as_tiles(fresh_key)
    fresh_v = as_tiles(fresh_value)
    stale_k = as_tiles(stale_key)
    stale_v = as_tiles(stale_value)

    def one_tile(index):
        listed = key_tiles[index].astype(jnp.int32)
        count = tile_count[index]
        same = (listed // per_patch) == (index // per_patch)
        keys = jnp.where(same[:, None, None, None], fresh_k[listed], stale_k[listed])
        values = jnp.where(same[:, None, None, None], fresh_v[listed], stale_v[listed])
        scores = jnp.einsum("qhd,sthd->hqst", query_t[index].astype(jnp.float32), keys.astype(jnp.float32)) * scale
        capped = soft_cap * jnp.tanh(scores / soft_cap)
        valid = jnp.arange(KEY_SLOTS, dtype=jnp.int32) < count
        weight = jnp.where(valid[None, None, :, None], jnp.exp(capped - soft_cap), jnp.float32(0.0))
        total = jnp.sum(weight, axis=(2, 3))
        weight_b = lax.optimization_barrier(weight.astype(jnp.bfloat16))
        numer = jnp.einsum("hqst,sthd->qhd", weight_b.astype(jnp.float32), values.astype(jnp.float32))
        return (numer / jnp.transpose(total)[:, :, None]).astype(jnp.bfloat16)

    result = lax.map(one_tile, jnp.arange(ALL_TILES, dtype=jnp.int32))
    return result.reshape(TOKENS, NUM_HEADS * HEAD_DIM)
```

```python
import functools

import jax
import jax.numpy as jnp
from jax import lax
from jax.experimental import pallas as pl
from jax.experimental.pallas import tpu as pltpu
from jax.sharding import PartitionSpec as P

NUM_HEADS = 16
HEAD_DIM = 128
TILE_TOKENS = 384
TILES_H = 2
TILES_W = 3
KEY_SLOTS = 18


soft_cap = 8.0


def with_halo(x, sides, width):
    for axis, dim in sides:
        size, length = (lax.axis_size(axis), x.shape[dim])
        up = [(i, (i + 1) % size) for i in range(size - 1)]
        down = [(j, i) for i, j in up]
        last = lax.slice_in_dim(x, length - width, length, axis=dim)
        leading = lax.slice_in_dim(x, 0, width, axis=dim)
        before = lax.ppermute(last, axis, up)
        after = lax.ppermute(leading, axis, down)
        x = jnp.concatenate([before, x, after], axis=dim)
    return x


def attention_kernel(local_heads, per_patch, ids_ref, count_ref, q_ref, kb_ref, kf_ref, ka_ref,
                     vb_ref, vf_ref, va_ref, o_ref, acc_ref, tot_ref):
    t = pl.program_id(0)
    factor = 1.0 / (HEAD_DIM**0.5) / soft_cap
    for h in range(local_heads):
        cols = slice(h * HEAD_DIM, (h + 1) * HEAD_DIM)
        query = q_ref[:, cols]
        acc_ref[...] = jnp.zeros_like(acc_ref)
        tot_ref[...] = jnp.zeros_like(tot_ref)

        def accumulate(k_ref, v_ref, row):
            start = pl.multiple_of(row * TILE_TOKENS, TILE_TOKENS)
            keys = k_ref[pl.ds(start, TILE_TOKENS), cols]
            values = v_ref[pl.ds(start, TILE_TOKENS), cols]
            scores = lax.dot_general(
                query, keys, (((1,), (1,)), ((), ())), preferred_element_type=jnp.float32
            )
            weight = jnp.exp(soft_cap * jnp.tanh(scores * factor) - soft_cap)
            part = weight[:, 0:HEAD_DIM]
            for c in range(1, TILE_TOKENS // HEAD_DIM):
                part = part + weight[:, c * HEAD_DIM:(c + 1) * HEAD_DIM]
            tot_ref[...] += part
            acc_ref[...] += jnp.dot(
                weight.astype(jnp.bfloat16), values, preferred_element_type=jnp.float32
            )

        def body(j, carry):
            u = ids_ref[t, j]
            which = u // per_patch
            row = u - which * per_patch

            @pl.when(which == 0)
            def _():
                accumulate(kb_ref, vb_ref, row)

            @pl.when(which == 1)
            def _():
                accumulate(kf_ref, vf_ref, row)

            @pl.when(which == 2)
            def _():
                accumulate(ka_ref, va_ref, row)

            return carry

        lax.fori_loop(0, count_ref[t], body, 0)
        total = jnp.sum(tot_ref[...], axis=1, keepdims=True)
        o_ref[:, cols] = (acc_ref[...] / total).astype(o_ref.dtype)


def tile_attention(q_heads, kb, kf, ka, vb, vf, va, local_ids, tile_count, local_heads, per_patch):
    rows, width = q_heads.shape
    tiles = rows // TILE_TOKENS
    whole = pl.BlockSpec((rows, width), lambda t, ids, cnt: (0, 0))
    tile = pl.BlockSpec((TILE_TOKENS, width), lambda t, ids, cnt: (t, 0))
    return pl.pallas_call(
        functools.partial(attention_kernel, local_heads, per_patch),
        out_shape=jax.ShapeDtypeStruct((rows, width), jnp.bfloat16),
        grid_spec=pltpu.PrefetchScalarGridSpec(
            num_scalar_prefetch=2,
            grid=(tiles,),
            in_specs=[tile, whole, whole, whole, whole, whole, whole],
            out_specs=tile,
            scratch_shapes=[
                pltpu.VMEM((TILE_TOKENS, HEAD_DIM), jnp.float32),
                pltpu.VMEM((TILE_TOKENS, HEAD_DIM), jnp.float32),
            ],
        ),
    )(local_ids, tile_count, q_heads, kb, kf, ka, vb, vf, va)


def on_device(query, fresh_key, fresh_value, stale_key, stale_value, key_tiles, tile_count):
    seq_count = lax.axis_size("seq")
    local_heads = NUM_HEADS // seq_count
    per_patch = TILES_H * TILES_W
    rows = query.shape[0]
    patch_rows = rows * seq_count
    q_heads, k_fresh, v_fresh = (
        lax.all_to_all(query, "seq", split_axis=1, concat_axis=0, tiled=True),
        lax.all_to_all(fresh_key, "seq", split_axis=1, concat_axis=0, tiled=True),
        lax.all_to_all(fresh_value, "seq", split_axis=1, concat_axis=0, tiled=True),
    )
    stale = jnp.stack([stale_key, stale_value])
    regrouped = lax.all_to_all(stale, "seq", split_axis=2, concat_axis=1, tiled=True)
    framed = with_halo(regrouped, (("patch", 1),), patch_rows)
    before = framed[:, :patch_rows]
    after = framed[:, 2 * patch_rows :]
    first_tile = (lax.axis_index("patch") - 1) * per_patch
    local_ids = (key_tiles - first_tile).astype(jnp.int32)
    merged = tile_attention(
        q_heads, before[0], k_fresh, after[0], before[1], v_fresh, after[1],
        local_ids, tile_count.astype(jnp.int32), local_heads, per_patch,
    )
    return lax.all_to_all(merged, "seq", split_axis=0, concat_axis=1, tiled=True)


def solution(mesh):
    return jax.shard_map(
        on_device,
        mesh=mesh,
        in_specs=(
            P(("cfg", "patch", "seq"), None),
            P(("cfg", "patch", "seq"), None),
            P(("cfg", "patch", "seq"), None),
            P(("cfg", "patch", "seq"), None),
            P(("cfg", "patch", "seq"), None),
            P("patch", None),
            P("patch"),
        ),
        out_specs=P(("cfg", "patch", "seq"), None),
        check_vma=False,
    )
```

```python
import functools

import jax
import jax.numpy as jnp
from jax import lax
from jax.experimental import pallas as pl
from jax.experimental.pallas import tpu as pltpu
from jax.sharding import PartitionSpec as P

NUM_HEADS = 16
HEAD_DIM = 128
TILE_TOKENS = 384
TILES_H = 2
TILES_W = 3
KEY_SLOTS = 18


soft_cap = 8.0


def with_halo(x, sides, width):
    for axis, dim in sides:
        size, length = (lax.axis_size(axis), x.shape[dim])
        up = [(i, (i + 1) % size) for i in range(size - 1)]
        down = [(j, i) for i, j in up]
        last = lax.slice_in_dim(x, length - width, length, axis=dim)
        leading = lax.slice_in_dim(x, 0, width, axis=dim)
        before = lax.ppermute(last, axis, up)
        after = lax.ppermute(leading, axis, down)
        x = jnp.concatenate([before, x, after], axis=dim)
    return x


def attention_kernel(local_heads, per_patch, ids_ref, count_ref, fresh_ref, before_ref, after_ref,
                     o_ref, acc_ref, tot_ref):
    t = pl.program_id(0)
    width = local_heads * HEAD_DIM
    factor = 1.0 / (HEAD_DIM**0.5) / soft_cap
    for h in range(local_heads):
        q_cols = pl.ds(2 * width + h * HEAD_DIM, HEAD_DIM)
        start_q = pl.multiple_of(t * TILE_TOKENS, TILE_TOKENS)
        query = fresh_ref[pl.ds(start_q, TILE_TOKENS), q_cols]
        acc_ref[...] = jnp.zeros_like(acc_ref)
        tot_ref[...] = jnp.zeros_like(tot_ref)

        def accumulate(ref, k_col, v_col, row):
            start = pl.multiple_of(row * TILE_TOKENS, TILE_TOKENS)
            keys = ref[pl.ds(start, TILE_TOKENS), pl.ds(k_col, HEAD_DIM)]
            values = ref[pl.ds(start, TILE_TOKENS), pl.ds(v_col, HEAD_DIM)]
            scores = lax.dot_general(
                query, keys, (((1,), (1,)), ((), ())), preferred_element_type=jnp.float32
            )
            weight = jnp.exp(soft_cap * jnp.tanh(scores * factor) - soft_cap)
            part = weight[:, 0:HEAD_DIM]
            for c in range(1, TILE_TOKENS // HEAD_DIM):
                part = part + weight[:, c * HEAD_DIM:(c + 1) * HEAD_DIM]
            tot_ref[...] += part
            acc_ref[...] += jnp.dot(
                weight.astype(jnp.bfloat16), values, preferred_element_type=jnp.float32
            )

        def body(j, carry):
            u = ids_ref[t, j]
            which = u // per_patch
            row = u - which * per_patch
            stale_k, stale_v = h * HEAD_DIM, width + h * HEAD_DIM

            @pl.when(which == 0)
            def _():
                accumulate(before_ref, stale_k, stale_v, row)

            @pl.when(which == 1)
            def _():
                accumulate(fresh_ref, 3 * width + h * HEAD_DIM, 4 * width + h * HEAD_DIM, row)

            @pl.when(which == 2)
            def _():
                accumulate(after_ref, stale_k, stale_v, row)

            return carry

        lax.fori_loop(0, count_ref[t], body, 0)
        total = jnp.sum(tot_ref[...], axis=1, keepdims=True)
        o_ref[:, pl.ds(h * HEAD_DIM, HEAD_DIM)] = (acc_ref[...] / total).astype(o_ref.dtype)


def tile_attention(fresh, before, after, local_ids, tile_count, local_heads, per_patch):
    rows = fresh.shape[0]
    width = local_heads * HEAD_DIM
    tiles = rows // TILE_TOKENS

    def whole(array):
        return pl.BlockSpec(array.shape, lambda t, ids, cnt: (0, 0))

    return pl.pallas_call(
        functools.partial(attention_kernel, local_heads, per_patch),
        out_shape=jax.ShapeDtypeStruct((rows, width), jnp.bfloat16),
        grid_spec=pltpu.PrefetchScalarGridSpec(
            num_scalar_prefetch=2,
            grid=(tiles,),
            in_specs=[whole(fresh), whole(before), whole(after)],
            out_specs=pl.BlockSpec((TILE_TOKENS, width), lambda t, ids, cnt: (t, 0)),
            scratch_shapes=[
                pltpu.VMEM((TILE_TOKENS, HEAD_DIM), jnp.float32),
                pltpu.VMEM((TILE_TOKENS, HEAD_DIM), jnp.float32),
            ],
        ),
    )(local_ids, tile_count, fresh, before, after)


def on_device(query, fresh_key, fresh_value, stale_key, stale_value, key_tiles, tile_count):
    seq_count = lax.axis_size("seq")
    local_heads = NUM_HEADS // seq_count
    width = local_heads * HEAD_DIM
    per_patch = TILES_H * TILES_W
    rows = query.shape[0]
    patch_rows = rows * seq_count
    stacked = jnp.stack([stale_key, stale_value, query, fresh_key, fresh_value], axis=1)
    stacked = stacked.reshape(rows, 5, seq_count, width)
    regrouped = lax.all_to_all(stacked, "seq", split_axis=2, concat_axis=0, tiled=True)
    fresh = regrouped.reshape(patch_rows, 5 * width)
    stale = fresh[:, : 2 * width]
    framed = with_halo(stale, (("patch", 0),), patch_rows)
    before = framed[:patch_rows]
    after = framed[2 * patch_rows :]
    first_tile = (lax.axis_index("patch") - 1) * per_patch
    local_ids = (key_tiles - first_tile).astype(jnp.int32)
    merged = tile_attention(
        fresh, before, after, local_ids, tile_count.astype(jnp.int32), local_heads, per_patch
    )
    return lax.all_to_all(merged, "seq", split_axis=0, concat_axis=1, tiled=True)


def solution(mesh):
    return jax.shard_map(
        on_device,
        mesh=mesh,
        in_specs=(
            P(("cfg", "patch", "seq"), None),
            P(("cfg", "patch", "seq"), None),
            P(("cfg", "patch", "seq"), None),
            P(("cfg", "patch", "seq"), None),
            P(("cfg", "patch", "seq"), None),
            P("patch", None),
            P("patch"),
        ),
        out_specs=P(("cfg", "patch", "seq"), None),
        check_vma=False,
    )
```

```python
import functools

import jax
import jax.numpy as jnp
from jax import lax
from jax.experimental import pallas as pl
from jax.experimental.pallas import tpu as pltpu
from jax.sharding import PartitionSpec as P

NUM_HEADS = 16
HEAD_DIM = 128
TILE_TOKENS = 384
TILES_H = 2
TILES_W = 3
KEY_SLOTS = 18


soft_cap = 8.0


def with_halo(x, sides, width):
    for axis, dim in sides:
        size, length = (lax.axis_size(axis), x.shape[dim])
        up = [(i, (i + 1) % size) for i in range(size - 1)]
        down = [(j, i) for i, j in up]
        last = lax.slice_in_dim(x, length - width, length, axis=dim)
        leading = lax.slice_in_dim(x, 0, width, axis=dim)
        before = lax.ppermute(last, axis, up)
        after = lax.ppermute(leading, axis, down)
        x = jnp.concatenate([before, x, after], axis=dim)
    return x


def attention_kernel(local_heads, per_patch, ids_ref, count_ref, fresh_ref, before_ref, after_ref,
                     o_ref, acc_ref, tot_ref):
    t = pl.program_id(0)
    width = local_heads * HEAD_DIM
    factor = 1.0 / (HEAD_DIM**0.5) / soft_cap
    for h in range(local_heads):
        q_cols = pl.ds(h * HEAD_DIM, HEAD_DIM)
        start_q = pl.multiple_of(t * TILE_TOKENS, TILE_TOKENS)
        query = fresh_ref[pl.ds(start_q, TILE_TOKENS), q_cols]
        acc_ref[...] = jnp.zeros_like(acc_ref)
        tot_ref[...] = jnp.zeros_like(tot_ref)

        def accumulate(ref, k_col, v_col, row):
            start = pl.multiple_of(row * TILE_TOKENS, TILE_TOKENS)
            keys = ref[pl.ds(start, TILE_TOKENS), pl.ds(k_col, HEAD_DIM)]
            values = ref[pl.ds(start, TILE_TOKENS), pl.ds(v_col, HEAD_DIM)]
            scores = lax.dot_general(
                query, keys, (((1,), (1,)), ((), ())), preferred_element_type=jnp.float32
            )
            weight = jnp.exp(soft_cap * jnp.tanh(scores * factor) - soft_cap)
            part = weight[:, 0:HEAD_DIM]
            for c in range(1, TILE_TOKENS // HEAD_DIM):
                part = part + weight[:, c * HEAD_DIM:(c + 1) * HEAD_DIM]
            tot_ref[...] += part
            acc_ref[...] += jnp.dot(
                weight.astype(jnp.bfloat16), values, preferred_element_type=jnp.float32
            )

        def body(j, carry):
            u = ids_ref[t, j]
            which = u // per_patch
            row = u - which * per_patch
            stale_k, stale_v = h * HEAD_DIM, width + h * HEAD_DIM

            @pl.when(which == 0)
            def _():
                accumulate(before_ref, stale_k, stale_v, row)

            @pl.when(which == 1)
            def _():
                accumulate(fresh_ref, width + h * HEAD_DIM, 2 * width + h * HEAD_DIM, row)

            @pl.when(which == 2)
            def _():
                accumulate(after_ref, stale_k, stale_v, row)

            return carry

        lax.fori_loop(0, count_ref[t], body, 0)
        total = jnp.sum(tot_ref[...], axis=1, keepdims=True)
        o_ref[:, pl.ds(h * HEAD_DIM, HEAD_DIM)] = (acc_ref[...] / total).astype(o_ref.dtype)


def tile_attention(fresh, before, after, local_ids, tile_count, local_heads, per_patch):
    rows = fresh.shape[0]
    width = local_heads * HEAD_DIM
    tiles = rows // TILE_TOKENS

    def whole(array):
        return pl.BlockSpec(array.shape, lambda t, ids, cnt: (0, 0))

    return pl.pallas_call(
        functools.partial(attention_kernel, local_heads, per_patch),
        out_shape=jax.ShapeDtypeStruct((rows, width), jnp.bfloat16),
        grid_spec=pltpu.PrefetchScalarGridSpec(
            num_scalar_prefetch=2,
            grid=(tiles,),
            in_specs=[whole(fresh), whole(before), whole(after)],
            out_specs=pl.BlockSpec((TILE_TOKENS, width), lambda t, ids, cnt: (t, 0)),
            scratch_shapes=[
                pltpu.VMEM((TILE_TOKENS, HEAD_DIM), jnp.float32),
                pltpu.VMEM((TILE_TOKENS, HEAD_DIM), jnp.float32),
            ],
        ),
    )(local_ids, tile_count, fresh, before, after)


def on_device(query, fresh_key, fresh_value, stale_key, stale_value, key_tiles, tile_count):
    seq_count = lax.axis_size("seq")
    local_heads = NUM_HEADS // seq_count
    width = local_heads * HEAD_DIM
    per_patch = TILES_H * TILES_W
    rows = query.shape[0]
    patch_rows = rows * seq_count
    stale = jnp.stack([stale_key, stale_value], axis=1).reshape(rows, 2, seq_count, width)
    stale = lax.all_to_all(stale, "seq", split_axis=2, concat_axis=0, tiled=True)
    stale = stale.reshape(patch_rows, 2 * width)
    framed = with_halo(stale, (("patch", 0),), patch_rows)
    before = framed[:patch_rows]
    after = framed[2 * patch_rows :]
    current = jnp.stack([query, fresh_key, fresh_value], axis=1).reshape(rows, 3, seq_count, width)
    current = lax.all_to_all(current, "seq", split_axis=2, concat_axis=0, tiled=True)
    fresh = current.reshape(patch_rows, 3 * width)
    first_tile = (lax.axis_index("patch") - 1) * per_patch
    local_ids = (key_tiles - first_tile).astype(jnp.int32)
    merged = tile_attention(
        fresh, before, after, local_ids, tile_count.astype(jnp.int32), local_heads, per_patch
    )
    return lax.all_to_all(merged, "seq", split_axis=0, concat_axis=1, tiled=True)


def solution(mesh):
    return jax.shard_map(
        on_device,
        mesh=mesh,
        in_specs=(
            P(("cfg", "patch", "seq"), None),
            P(("cfg", "patch", "seq"), None),
            P(("cfg", "patch", "seq"), None),
            P(("cfg", "patch", "seq"), None),
            P(("cfg", "patch", "seq"), None),
            P("patch", None),
            P("patch"),
        ),
        out_specs=P(("cfg", "patch", "seq"), None),
        check_vma=False,
    )
```

```python
import functools

import jax
import jax.numpy as jnp
from jax import lax
from jax.experimental import pallas as pl
from jax.experimental.pallas import tpu as pltpu
from jax.sharding import PartitionSpec as P

NUM_HEADS = 16
HEAD_DIM = 128
TILE_TOKENS = 384
TILES_H = 2
TILES_W = 3
KEY_SLOTS = 18


soft_cap = 8.0


def with_halo(x, sides, width):
    for axis, dim in sides:
        size, length = (lax.axis_size(axis), x.shape[dim])
        up = [(i, (i + 1) % size) for i in range(size - 1)]
        down = [(j, i) for i, j in up]
        last = lax.slice_in_dim(x, length - width, length, axis=dim)
        leading = lax.slice_in_dim(x, 0, width, axis=dim)
        before = lax.ppermute(last, axis, up)
        after = lax.ppermute(leading, axis, down)
        x = jnp.concatenate([before, x, after], axis=dim)
    return x


def attention_kernel(local_heads, per_patch, stale_phase, ids_ref, count_ref, fresh_ref, *refs):
    if stale_phase:
        before_ref, after_ref, acc_in, tot_in, o_ref, acc_ref, tot_ref = refs
    else:
        acc_ref, tot_ref = refs
    t = pl.program_id(0)
    width = local_heads * HEAD_DIM
    factor = 1.0 / (HEAD_DIM**0.5) / soft_cap
    for h in range(local_heads):
        head = pl.ds(h * HEAD_DIM, HEAD_DIM)
        start_q = pl.multiple_of(t * TILE_TOKENS, TILE_TOKENS)
        query = fresh_ref[pl.ds(start_q, TILE_TOKENS), pl.ds(h * 3 * HEAD_DIM, HEAD_DIM)]
        if stale_phase:
            acc_ref[...] = acc_in[:, head]
            tot_ref[...] = tot_in[:, head]
        else:
            acc_ref[:, head] = jnp.zeros((TILE_TOKENS, HEAD_DIM), jnp.float32)
            tot_ref[:, head] = jnp.zeros((TILE_TOKENS, HEAD_DIM), jnp.float32)
        acc_at = slice(None) if stale_phase else head

        def accumulate(ref, k_col, v_col, row):
            start = pl.multiple_of(row * TILE_TOKENS, TILE_TOKENS)
            keys = ref[pl.ds(start, TILE_TOKENS), pl.ds(k_col, HEAD_DIM)]
            values = ref[pl.ds(start, TILE_TOKENS), pl.ds(v_col, HEAD_DIM)]
            scores = lax.dot_general(
                query, keys, (((1,), (1,)), ((), ())), preferred_element_type=jnp.float32
            )
            weight = jnp.exp(soft_cap * jnp.tanh(scores * factor) - soft_cap)
            part = weight[:, 0:HEAD_DIM]
            for c in range(1, TILE_TOKENS // HEAD_DIM):
                part = part + weight[:, c * HEAD_DIM:(c + 1) * HEAD_DIM]
            tot_ref[:, acc_at] += part
            acc_ref[:, acc_at] += jnp.dot(
                weight.astype(jnp.bfloat16), values, preferred_element_type=jnp.float32
            )

        def body(j, carry):
            u = ids_ref[t, j]
            which = u // per_patch
            row = u - which * per_patch
            if stale_phase:
                stale_k, stale_v = h * 2 * HEAD_DIM, (h * 2 + 1) * HEAD_DIM

                @pl.when(which == 0)
                def _():
                    accumulate(before_ref, stale_k, stale_v, row)

                @pl.when(which == 2)
                def _():
                    accumulate(after_ref, stale_k, stale_v, row)
            else:

                @pl.when(which == 1)
                def _():
                    accumulate(fresh_ref, (h * 3 + 1) * HEAD_DIM, (h * 3 + 2) * HEAD_DIM, row)

            return carry

        lax.fori_loop(0, count_ref[t], body, 0)
        if stale_phase:
            total = jnp.sum(tot_ref[...], axis=1, keepdims=True)
            o_ref[:, head] = (acc_ref[...] / total).astype(o_ref.dtype)


def tile_attention(fresh, before, after, local_ids, tile_count, local_heads, per_patch):
    rows = fresh.shape[0]
    width = local_heads * HEAD_DIM
    tiles = rows // TILE_TOKENS

    def whole(array):
        return pl.BlockSpec(array.shape, lambda t, ids, cnt: (0, 0))

    tile = pl.BlockSpec((TILE_TOKENS, width), lambda t, ids, cnt: (t, 0))
    partial = jax.ShapeDtypeStruct((rows, width), jnp.float32)
    acc, tot = pl.pallas_call(
        functools.partial(attention_kernel, local_heads, per_patch, False),
        out_shape=(partial, partial),
        grid_spec=pltpu.PrefetchScalarGridSpec(
            num_scalar_prefetch=2, grid=(tiles,), in_specs=[whole(fresh)], out_specs=(tile, tile),
        ),
    )(local_ids, tile_count, fresh)
    return pl.pallas_call(
        functools.partial(attention_kernel, local_heads, per_patch, True),
        out_shape=jax.ShapeDtypeStruct((rows, width), jnp.bfloat16),
        grid_spec=pltpu.PrefetchScalarGridSpec(
            num_scalar_prefetch=2,
            grid=(tiles,),
            in_specs=[whole(fresh), whole(before), whole(after), tile, tile],
            out_specs=tile,
            scratch_shapes=[
                pltpu.VMEM((TILE_TOKENS, HEAD_DIM), jnp.float32),
                pltpu.VMEM((TILE_TOKENS, HEAD_DIM), jnp.float32),
            ],
        ),
    )(local_ids, tile_count, fresh, before, after, acc, tot)


def on_device(query, fresh_key, fresh_value, stale_key, stale_value, key_tiles, tile_count):
    seq_count = lax.axis_size("seq")
    local_heads = NUM_HEADS // seq_count
    width = local_heads * HEAD_DIM
    per_patch = TILES_H * TILES_W
    rows = query.shape[0]
    patch_rows = rows * seq_count

    def interleaved(arrays):
        parts = [a.reshape(rows, NUM_HEADS, HEAD_DIM) for a in arrays]
        joined = jnp.stack(parts, axis=2).reshape(rows, NUM_HEADS * len(arrays) * HEAD_DIM)
        return lax.all_to_all(joined, "seq", split_axis=1, concat_axis=0, tiled=True)

    stale = interleaved([stale_key, stale_value])
    framed = with_halo(stale, (("patch", 0),), patch_rows)
    before = framed[:patch_rows]
    after = framed[2 * patch_rows :]
    fresh = interleaved([query, fresh_key, fresh_value])
    first_tile = (lax.axis_index("patch") - 1) * per_patch
    local_ids = (key_tiles - first_tile).astype(jnp.int32)
    merged = tile_attention(
        fresh, before, after, local_ids, tile_count.astype(jnp.int32), local_heads, per_patch
    )
    return lax.all_to_all(merged, "seq", split_axis=0, concat_axis=1, tiled=True)


def solution(mesh):
    return jax.shard_map(
        on_device,
        mesh=mesh,
        in_specs=(
            P(("cfg", "patch", "seq"), None),
            P(("cfg", "patch", "seq"), None),
            P(("cfg", "patch", "seq"), None),
            P(("cfg", "patch", "seq"), None),
            P(("cfg", "patch", "seq"), None),
            P("patch", None),
            P("patch"),
        ),
        out_specs=P(("cfg", "patch", "seq"), None),
        check_vma=False,
    )
```

```python
import functools

import jax
import jax.numpy as jnp
from jax import lax
from jax.experimental import pallas as pl
from jax.experimental.pallas import tpu as pltpu
from jax.sharding import PartitionSpec as P

NUM_HEADS = 16
HEAD_DIM = 128
TILE_TOKENS = 384
TILES_H = 2
TILES_W = 3
KEY_SLOTS = 18


soft_cap = 8.0


def with_halo(x, sides, width):
    for axis, dim in sides:
        size, length = (lax.axis_size(axis), x.shape[dim])
        up = [(i, (i + 1) % size) for i in range(size - 1)]
        down = [(j, i) for i, j in up]
        last = lax.slice_in_dim(x, length - width, length, axis=dim)
        leading = lax.slice_in_dim(x, 0, width, axis=dim)
        before = lax.ppermute(last, axis, up)
        after = lax.ppermute(leading, axis, down)
        x = jnp.concatenate([before, x, after], axis=dim)
    return x


def attention_kernel(local_heads, per_patch, stale_phase, ids_ref, count_ref, fresh_ref, *refs):
    if stale_phase:
        before_ref, after_ref, acc_in, tot_in, o_ref, acc_ref, tot_ref = refs
    else:
        acc_ref, tot_ref = refs
    t = pl.program_id(0)
    width = local_heads * HEAD_DIM
    factor = 1.0 / (HEAD_DIM**0.5) / soft_cap
    for h in range(local_heads):
        head = pl.ds(h * HEAD_DIM, HEAD_DIM)
        start_q = pl.multiple_of(t * TILE_TOKENS, TILE_TOKENS)
        query = fresh_ref[pl.ds(start_q, TILE_TOKENS), pl.ds(h * HEAD_DIM, HEAD_DIM)]
        if stale_phase:
            acc_ref[...] = acc_in[:, head]
            tot_ref[...] = tot_in[:, head]
        else:
            acc_ref[:, head] = jnp.zeros((TILE_TOKENS, HEAD_DIM), jnp.float32)
            tot_ref[:, head] = jnp.zeros((TILE_TOKENS, HEAD_DIM), jnp.float32)
        acc_at = slice(None) if stale_phase else head

        def accumulate(ref, k_col, v_col, row):
            start = pl.multiple_of(row * TILE_TOKENS, TILE_TOKENS)
            keys = ref[pl.ds(start, TILE_TOKENS), pl.ds(k_col, HEAD_DIM)]
            values = ref[pl.ds(start, TILE_TOKENS), pl.ds(v_col, HEAD_DIM)]
            scores = lax.dot_general(
                query, keys, (((1,), (1,)), ((), ())), preferred_element_type=jnp.float32
            )
            weight = jnp.exp(soft_cap * jnp.tanh(scores * factor) - soft_cap)
            part = weight[:, 0:HEAD_DIM]
            for c in range(1, TILE_TOKENS // HEAD_DIM):
                part = part + weight[:, c * HEAD_DIM:(c + 1) * HEAD_DIM]
            tot_ref[:, acc_at] += part
            acc_ref[:, acc_at] += jnp.dot(
                weight.astype(jnp.bfloat16), values, preferred_element_type=jnp.float32
            )

        def body(j, carry):
            u = ids_ref[t, j]
            which = u // per_patch
            row = u - which * per_patch
            if stale_phase:
                stale_k, stale_v = h * HEAD_DIM, width + h * HEAD_DIM

                @pl.when(which == 0)
                def _():
                    accumulate(before_ref, stale_k, stale_v, row)

                @pl.when(which == 2)
                def _():
                    accumulate(after_ref, stale_k, stale_v, row)
            else:

                @pl.when(which == 1)
                def _():
                    accumulate(fresh_ref, width + h * HEAD_DIM, 2 * width + h * HEAD_DIM, row)

            return carry

        lax.fori_loop(0, count_ref[t], body, 0)
        if stale_phase:
            total = jnp.sum(tot_ref[...], axis=1, keepdims=True)
            o_ref[:, head] = (acc_ref[...] / total).astype(o_ref.dtype)


def tile_attention(fresh, before, after, local_ids, tile_count, local_heads, per_patch):
    rows = fresh.shape[0]
    width = local_heads * HEAD_DIM
    tiles = rows // TILE_TOKENS

    def whole(array):
        return pl.BlockSpec(array.shape, lambda t, ids, cnt: (0, 0))

    tile = pl.BlockSpec((TILE_TOKENS, width), lambda t, ids, cnt: (t, 0))
    partial = jax.ShapeDtypeStruct((rows, width), jnp.float32)
    acc, tot = pl.pallas_call(
        functools.partial(attention_kernel, local_heads, per_patch, False),
        out_shape=(partial, partial),
        grid_spec=pltpu.PrefetchScalarGridSpec(
            num_scalar_prefetch=2, grid=(tiles,), in_specs=[whole(fresh)], out_specs=(tile, tile),
        ),
    )(local_ids, tile_count, fresh)
    return pl.pallas_call(
        functools.partial(attention_kernel, local_heads, per_patch, True),
        out_shape=jax.ShapeDtypeStruct((rows, width), jnp.bfloat16),
        grid_spec=pltpu.PrefetchScalarGridSpec(
            num_scalar_prefetch=2,
            grid=(tiles,),
            in_specs=[whole(fresh), whole(before), whole(after), tile, tile],
            out_specs=tile,
            scratch_shapes=[
                pltpu.VMEM((TILE_TOKENS, HEAD_DIM), jnp.float32),
                pltpu.VMEM((TILE_TOKENS, HEAD_DIM), jnp.float32),
            ],
        ),
    )(local_ids, tile_count, fresh, before, after, acc, tot)


def on_device(query, fresh_key, fresh_value, stale_key, stale_value, key_tiles, tile_count):
    seq_count = lax.axis_size("seq")
    local_heads = NUM_HEADS // seq_count
    width = local_heads * HEAD_DIM
    per_patch = TILES_H * TILES_W
    rows = query.shape[0]
    patch_rows = rows * seq_count

    def interleaved(arrays):
        parts = [a.reshape(rows, seq_count, width) for a in arrays]
        joined = jnp.concatenate(parts, axis=2).transpose(1, 0, 2)
        moved = lax.all_to_all(joined, "seq", split_axis=0, concat_axis=0, tiled=True)
        return moved.reshape(patch_rows, len(arrays) * width)

    stale = interleaved([stale_key, stale_value])
    framed = with_halo(stale, (("patch", 0),), patch_rows)
    before = framed[:patch_rows]
    after = framed[2 * patch_rows :]
    fresh = interleaved([query, fresh_key, fresh_value])
    first_tile = (lax.axis_index("patch") - 1) * per_patch
    local_ids = (key_tiles - first_tile).astype(jnp.int32)
    merged = tile_attention(
        fresh, before, after, local_ids, tile_count.astype(jnp.int32), local_heads, per_patch
    )
    return lax.all_to_all(merged, "seq", split_axis=0, concat_axis=1, tiled=True)


def solution(mesh):
    return jax.shard_map(
        on_device,
        mesh=mesh,
        in_specs=(
            P(("cfg", "patch", "seq"), None),
            P(("cfg", "patch", "seq"), None),
            P(("cfg", "patch", "seq"), None),
            P(("cfg", "patch", "seq"), None),
            P(("cfg", "patch", "seq"), None),
            P("patch", None),
            P("patch"),
        ),
        out_specs=P(("cfg", "patch", "seq"), None),
        check_vma=False,
    )
```

```python
import functools

import jax
import jax.numpy as jnp
from jax import lax
from jax.experimental import pallas as pl
from jax.experimental.pallas import tpu as pltpu
from jax.sharding import PartitionSpec as P

NUM_HEADS = 16
HEAD_DIM = 128
TILE_TOKENS = 384
TILES_H = 2
TILES_W = 3
KEY_SLOTS = 18


soft_cap = 8.0


def with_halo(x, sides, width):
    for axis, dim in sides:
        size, length = (lax.axis_size(axis), x.shape[dim])
        up = [(i, (i + 1) % size) for i in range(size - 1)]
        down = [(j, i) for i, j in up]
        last = lax.slice_in_dim(x, length - width, length, axis=dim)
        leading = lax.slice_in_dim(x, 0, width, axis=dim)
        before = lax.ppermute(last, axis, up)
        after = lax.ppermute(leading, axis, down)
        x = jnp.concatenate([before, x, after], axis=dim)
    return x


def attention_kernel(local_heads, per_patch, stale_phase, ids_ref, count_ref, fresh_ref, *refs):
    if stale_phase:
        before_hbm, after_hbm, acc_in, tot_in, o_ref, stale_ref, copy_sem, list_ref, acc_ref, tot_ref = refs
        keys_ref = stale_ref
    else:
        acc_ref, tot_ref, list_ref = refs
        keys_ref = fresh_ref
    t = pl.program_id(0)
    width = local_heads * HEAD_DIM
    patch_rows = fresh_ref.shape[0]
    factor = 1.0 / (HEAD_DIM**0.5) / soft_cap
    lift = soft_cap * 1.4426950408889634

    if stale_phase:

        @pl.when(t == 0)
        def _():
            first = pltpu.make_async_copy(before_hbm, stale_ref.at[pl.ds(0, patch_rows)], copy_sem.at[0])
            second = pltpu.make_async_copy(
                after_hbm, stale_ref.at[pl.ds(patch_rows, patch_rows)], copy_sem.at[1]
            )
            first.start()
            second.start()
            first.wait()
            second.wait()

    def compact(j, n):
        u = ids_ref[t, j]
        which = u // per_patch
        row = u - which * per_patch
        if stale_phase:
            keep = which != 1
            index = (which // 2) * per_patch + row
        else:
            keep = which == 1
            index = row

        @pl.when(keep)
        def _():
            list_ref[n] = index

        return n + keep.astype(jnp.int32)

    used = lax.fori_loop(0, count_ref[t], compact, jnp.int32(0))

    for h in range(local_heads):
        head = pl.ds(h * HEAD_DIM, HEAD_DIM)
        start_q = pl.multiple_of(t * TILE_TOKENS, TILE_TOKENS)
        query = fresh_ref[pl.ds(start_q, TILE_TOKENS), pl.ds(h * HEAD_DIM, HEAD_DIM)]
        if stale_phase:
            acc_ref[...] = acc_in[:, head]
            tot_ref[...] = tot_in[:, head]
            k_col, v_col = h * HEAD_DIM, width + h * HEAD_DIM
        else:
            acc_ref[:, head] = jnp.zeros((TILE_TOKENS, HEAD_DIM), jnp.float32)
            tot_ref[:, head] = jnp.zeros((TILE_TOKENS, HEAD_DIM), jnp.float32)
            k_col, v_col = width + h * HEAD_DIM, 2 * width + h * HEAD_DIM
        acc_at = slice(None) if stale_phase else head

        def weights(index):
            start = pl.multiple_of(index * TILE_TOKENS, TILE_TOKENS)
            keys = keys_ref[pl.ds(start, TILE_TOKENS), pl.ds(k_col, HEAD_DIM)]
            values = keys_ref[pl.ds(start, TILE_TOKENS), pl.ds(v_col, HEAD_DIM)]
            scores = lax.dot_general(
                query, keys, (((1,), (1,)), ((), ())), preferred_element_type=jnp.float32
            )
            weight = jnp.exp2(jnp.tanh(scores * factor) * lift - lift)
            part = weight[:, 0:HEAD_DIM]
            for c in range(1, TILE_TOKENS // HEAD_DIM):
                part = part + weight[:, c * HEAD_DIM:(c + 1) * HEAD_DIM]
            return weight.astype(jnp.bfloat16), part, values

        def accumulate(indices):
            got = [weights(i) for i in indices]
            part = got[0][1]
            for g in got[1:]:
                part = part + g[1]
            tot_ref[:, acc_at] += part
            acc_ref[:, acc_at] += jnp.dot(
                jnp.concatenate([g[0] for g in got], axis=1),
                jnp.concatenate([g[2] for g in got], axis=0),
                preferred_element_type=jnp.float32,
            )

        def two(p, carry):
            accumulate([list_ref[2 * p], list_ref[2 * p + 1]])
            return carry

        lax.fori_loop(0, used // 2, two, 0)

        @pl.when(used % 2 == 1)
        def _():
            accumulate([list_ref[used - 1]])

        if stale_phase:
            total = jnp.sum(tot_ref[...], axis=1, keepdims=True)
            o_ref[:, head] = (acc_ref[...] / total).astype(o_ref.dtype)


def tile_attention(fresh, before, after, local_ids, tile_count, local_heads, per_patch):
    rows = fresh.shape[0]
    width = local_heads * HEAD_DIM
    tiles = rows // TILE_TOKENS

    def whole(array):
        return pl.BlockSpec(array.shape, lambda t, ids, cnt: (0, 0))

    tile = pl.BlockSpec((TILE_TOKENS, width), lambda t, ids, cnt: (t, 0))
    partial = jax.ShapeDtypeStruct((rows, width), jnp.float32)
    acc, tot = pl.pallas_call(
        functools.partial(attention_kernel, local_heads, per_patch, False),
        out_shape=(partial, partial),
        grid_spec=pltpu.PrefetchScalarGridSpec(
            num_scalar_prefetch=2,
            grid=(tiles,),
            in_specs=[whole(fresh)],
            out_specs=(tile, tile),
            scratch_shapes=[pltpu.SMEM((KEY_SLOTS,), jnp.int32)],
        ),
    )(local_ids, tile_count, fresh)
    hbm = pl.BlockSpec(memory_space=pl.ANY)
    return pl.pallas_call(
        functools.partial(attention_kernel, local_heads, per_patch, True),
        out_shape=jax.ShapeDtypeStruct((rows, width), jnp.bfloat16),
        grid_spec=pltpu.PrefetchScalarGridSpec(
            num_scalar_prefetch=2,
            grid=(tiles,),
            in_specs=[whole(fresh), hbm, hbm, tile, tile],
            out_specs=tile,
            scratch_shapes=[
                pltpu.VMEM((2 * rows, before.shape[1]), before.dtype),
                pltpu.SemaphoreType.DMA((2,)),
                pltpu.SMEM((KEY_SLOTS,), jnp.int32),
                pltpu.VMEM((TILE_TOKENS, HEAD_DIM), jnp.float32),
                pltpu.VMEM((TILE_TOKENS, HEAD_DIM), jnp.float32),
            ],
        ),
        compiler_params=pltpu.CompilerParams(dimension_semantics=("arbitrary",)),
    )(local_ids, tile_count, fresh, before, after, acc, tot)


def on_device(query, fresh_key, fresh_value, stale_key, stale_value, key_tiles, tile_count):
    seq_count = lax.axis_size("seq")
    local_heads = NUM_HEADS // seq_count
    width = local_heads * HEAD_DIM
    per_patch = TILES_H * TILES_W
    rows = query.shape[0]
    patch_rows = rows * seq_count

    def interleaved(arrays):
        parts = [a.reshape(rows, seq_count, width) for a in arrays]
        joined = jnp.concatenate(parts, axis=2).transpose(1, 0, 2)
        moved = lax.all_to_all(joined, "seq", split_axis=0, concat_axis=0, tiled=True)
        return moved.reshape(patch_rows, len(arrays) * width)

    stale = interleaved([stale_key, stale_value])
    framed = with_halo(stale, (("patch", 0),), patch_rows)
    before = framed[:patch_rows]
    after = framed[2 * patch_rows :]
    fresh = interleaved([query, fresh_key, fresh_value])
    first_tile = (lax.axis_index("patch") - 1) * per_patch
    local_ids = (key_tiles - first_tile).astype(jnp.int32)
    merged = tile_attention(
        fresh, before, after, local_ids, tile_count.astype(jnp.int32), local_heads, per_patch
    )
    return lax.all_to_all(merged, "seq", split_axis=0, concat_axis=1, tiled=True)


def solution(mesh):
    return jax.shard_map(
        on_device,
        mesh=mesh,
        in_specs=(
            P(("cfg", "patch", "seq"), None),
            P(("cfg", "patch", "seq"), None),
            P(("cfg", "patch", "seq"), None),
            P(("cfg", "patch", "seq"), None),
            P(("cfg", "patch", "seq"), None),
            P("patch", None),
            P("patch"),
        ),
        out_specs=P(("cfg", "patch", "seq"), None),
        check_vma=False,
    )
```

```python
import functools

import jax
import jax.numpy as jnp
from jax import lax
from jax.experimental import pallas as pl
from jax.experimental.pallas import tpu as pltpu
from jax.sharding import PartitionSpec as P

NUM_HEADS = 16
HEAD_DIM = 128
TILE_TOKENS = 384
TILES_H = 2
TILES_W = 3
KEY_SLOTS = 18
SLOT_GROUP = 3


soft_cap = 8.0


def with_halo(x, sides, width):
    for axis, dim in sides:
        size, length = (lax.axis_size(axis), x.shape[dim])
        up = [(i, (i + 1) % size) for i in range(size - 1)]
        down = [(j, i) for i, j in up]
        last = lax.slice_in_dim(x, length - width, length, axis=dim)
        leading = lax.slice_in_dim(x, 0, width, axis=dim)
        before = lax.ppermute(last, axis, up)
        after = lax.ppermute(leading, axis, down)
        x = jnp.concatenate([before, x, after], axis=dim)
    return x


def attention_kernel(local_heads, per_patch, stale_phase, ids_ref, count_ref, fresh_ref, *refs):
    if stale_phase:
        before_hbm, after_hbm, acc_in, tot_in, o_ref, stale_ref, copy_sem, list_ref, acc_ref, tot_ref = refs
        keys_ref = stale_ref
    else:
        acc_ref, tot_ref, list_ref = refs
        keys_ref = fresh_ref
    t = pl.program_id(0)
    width = local_heads * HEAD_DIM
    patch_rows = fresh_ref.shape[0]
    factor = 1.0 / (HEAD_DIM**0.5) / soft_cap
    lift = soft_cap * 1.4426950408889634

    if stale_phase:

        @pl.when(t == 0)
        def _():
            first = pltpu.make_async_copy(before_hbm, stale_ref.at[pl.ds(0, patch_rows)], copy_sem.at[0])
            second = pltpu.make_async_copy(
                after_hbm, stale_ref.at[pl.ds(patch_rows, patch_rows)], copy_sem.at[1]
            )
            first.start()
            second.start()
            first.wait()
            second.wait()

    def compact(j, n):
        u = ids_ref[t, j]
        which = u // per_patch
        row = u - which * per_patch
        if stale_phase:
            keep = which != 1
            index = (which // 2) * per_patch + row
        else:
            keep = which == 1
            index = row

        @pl.when(keep)
        def _():
            list_ref[n] = index

        return n + keep.astype(jnp.int32)

    used = lax.fori_loop(0, count_ref[t], compact, jnp.int32(0))

    for h in range(local_heads):
        head = pl.ds(h * HEAD_DIM, HEAD_DIM)
        start_q = pl.multiple_of(t * TILE_TOKENS, TILE_TOKENS)
        query = fresh_ref[pl.ds(start_q, TILE_TOKENS), pl.ds(h * HEAD_DIM, HEAD_DIM)]
        if stale_phase:
            acc_ref[...] = acc_in[:, head]
            tot_ref[...] = tot_in[:, head]
            k_col, v_col = h * HEAD_DIM, width + h * HEAD_DIM
        else:
            acc_ref[:, head] = jnp.zeros((TILE_TOKENS, HEAD_DIM), jnp.float32)
            tot_ref[:, head] = jnp.zeros((TILE_TOKENS, HEAD_DIM), jnp.float32)
            k_col, v_col = width + h * HEAD_DIM, 2 * width + h * HEAD_DIM
        acc_at = slice(None) if stale_phase else head

        def weights(index):
            start = pl.multiple_of(index * TILE_TOKENS, TILE_TOKENS)
            keys = keys_ref[pl.ds(start, TILE_TOKENS), pl.ds(k_col, HEAD_DIM)]
            values = keys_ref[pl.ds(start, TILE_TOKENS), pl.ds(v_col, HEAD_DIM)]
            scores = lax.dot_general(
                query, keys, (((1,), (1,)), ((), ())), preferred_element_type=jnp.float32
            )
            weight = jnp.exp2(jnp.tanh(scores * factor) * lift - lift)
            part = weight[:, 0:HEAD_DIM]
            for c in range(1, TILE_TOKENS // HEAD_DIM):
                part = part + weight[:, c * HEAD_DIM:(c + 1) * HEAD_DIM]
            return weight.astype(jnp.bfloat16), part, values

        def accumulate(indices):
            got = [weights(i) for i in indices]
            part = got[0][1]
            for g in got[1:]:
                part = part + g[1]
            tot_ref[:, acc_at] += part
            acc_ref[:, acc_at] += jnp.dot(
                jnp.concatenate([g[0] for g in got], axis=1),
                jnp.concatenate([g[2] for g in got], axis=0),
                preferred_element_type=jnp.float32,
            )

        def group(p, carry):
            accumulate([list_ref[SLOT_GROUP * p + i] for i in range(SLOT_GROUP)])
            return carry

        lax.fori_loop(0, used // SLOT_GROUP, group, 0)
        for left in range(1, SLOT_GROUP):

            @pl.when(used % SLOT_GROUP == left)
            def _():
                accumulate([list_ref[used - left + i] for i in range(left)])

        if stale_phase:
            total = jnp.sum(tot_ref[...], axis=1, keepdims=True)
            o_ref[:, head] = (acc_ref[...] / total).astype(o_ref.dtype)


def tile_attention(fresh, before, after, local_ids, tile_count, local_heads, per_patch):
    rows = fresh.shape[0]
    width = local_heads * HEAD_DIM
    tiles = rows // TILE_TOKENS

    def whole(array):
        return pl.BlockSpec(array.shape, lambda t, ids, cnt: (0, 0))

    tile = pl.BlockSpec((TILE_TOKENS, width), lambda t, ids, cnt: (t, 0))
    partial = jax.ShapeDtypeStruct((rows, width), jnp.float32)
    acc, tot = pl.pallas_call(
        functools.partial(attention_kernel, local_heads, per_patch, False),
        out_shape=(partial, partial),
        grid_spec=pltpu.PrefetchScalarGridSpec(
            num_scalar_prefetch=2,
            grid=(tiles,),
            in_specs=[whole(fresh)],
            out_specs=(tile, tile),
            scratch_shapes=[pltpu.SMEM((KEY_SLOTS,), jnp.int32)],
        ),
    )(local_ids, tile_count, fresh)
    hbm = pl.BlockSpec(memory_space=pl.ANY)
    return pl.pallas_call(
        functools.partial(attention_kernel, local_heads, per_patch, True),
        out_shape=jax.ShapeDtypeStruct((rows, width), jnp.bfloat16),
        grid_spec=pltpu.PrefetchScalarGridSpec(
            num_scalar_prefetch=2,
            grid=(tiles,),
            in_specs=[whole(fresh), hbm, hbm, tile, tile],
            out_specs=tile,
            scratch_shapes=[
                pltpu.VMEM((2 * rows, before.shape[1]), before.dtype),
                pltpu.SemaphoreType.DMA((2,)),
                pltpu.SMEM((KEY_SLOTS,), jnp.int32),
                pltpu.VMEM((TILE_TOKENS, HEAD_DIM), jnp.float32),
                pltpu.VMEM((TILE_TOKENS, HEAD_DIM), jnp.float32),
            ],
        ),
        compiler_params=pltpu.CompilerParams(dimension_semantics=("arbitrary",)),
    )(local_ids, tile_count, fresh, before, after, acc, tot)


def on_device(query, fresh_key, fresh_value, stale_key, stale_value, key_tiles, tile_count):
    seq_count = lax.axis_size("seq")
    local_heads = NUM_HEADS // seq_count
    width = local_heads * HEAD_DIM
    per_patch = TILES_H * TILES_W
    rows = query.shape[0]
    patch_rows = rows * seq_count

    def interleaved(arrays):
        parts = [a.reshape(rows, seq_count, width) for a in arrays]
        joined = jnp.concatenate(parts, axis=2).transpose(1, 0, 2)
        moved = lax.all_to_all(joined, "seq", split_axis=0, concat_axis=0, tiled=True)
        return moved.reshape(patch_rows, len(arrays) * width)

    stale = interleaved([stale_key, stale_value])
    framed = with_halo(stale, (("patch", 0),), patch_rows)
    before = framed[:patch_rows]
    after = framed[2 * patch_rows :]
    fresh = interleaved([query, fresh_key, fresh_value])
    first_tile = (lax.axis_index("patch") - 1) * per_patch
    local_ids = (key_tiles - first_tile).astype(jnp.int32)
    merged = tile_attention(
        fresh, before, after, local_ids, tile_count.astype(jnp.int32), local_heads, per_patch
    )
    return lax.all_to_all(merged, "seq", split_axis=0, concat_axis=1, tiled=True)


def solution(mesh):
    return jax.shard_map(
        on_device,
        mesh=mesh,
        in_specs=(
            P(("cfg", "patch", "seq"), None),
            P(("cfg", "patch", "seq"), None),
            P(("cfg", "patch", "seq"), None),
            P(("cfg", "patch", "seq"), None),
            P(("cfg", "patch", "seq"), None),
            P("patch", None),
            P("patch"),
        ),
        out_specs=P(("cfg", "patch", "seq"), None),
        check_vma=False,
    )
```

```python
import functools

import jax
import jax.numpy as jnp
from jax import lax
from jax.experimental import pallas as pl
from jax.experimental.pallas import tpu as pltpu
from jax.sharding import PartitionSpec as P

NUM_HEADS = 16
HEAD_DIM = 128
TILE_TOKENS = 384
TILES_H = 2
TILES_W = 3
KEY_SLOTS = 18
SLOT_GROUP = 3


soft_cap = 8.0


def with_halo(x, sides, width):
    for axis, dim in sides:
        size, length = (lax.axis_size(axis), x.shape[dim])
        up = [(i, (i + 1) % size) for i in range(size - 1)]
        down = [(j, i) for i, j in up]
        last = lax.slice_in_dim(x, length - width, length, axis=dim)
        leading = lax.slice_in_dim(x, 0, width, axis=dim)
        before = lax.ppermute(last, axis, up)
        after = lax.ppermute(leading, axis, down)
        x = jnp.concatenate([before, x, after], axis=dim)
    return x


def attention_kernel(local_heads, per_patch, stale_phase, ids_ref, count_ref, fresh_ref, *refs):
    if stale_phase:
        before_hbm, after_hbm, acc_in, tot_in, o_ref, stale_ref, copy_sem, list_ref, acc_ref, tot_ref = refs
        keys_ref = stale_ref
    else:
        acc_ref, tot_ref, list_ref = refs
        keys_ref = fresh_ref
    t = pl.program_id(0)
    width = local_heads * HEAD_DIM
    patch_rows = fresh_ref.shape[0]
    factor = 1.0 / (HEAD_DIM**0.5) / soft_cap
    lift = soft_cap * 1.4426950408889634

    if stale_phase:

        @pl.when(t == 0)
        def _():
            first = pltpu.make_async_copy(before_hbm, stale_ref.at[pl.ds(0, patch_rows)], copy_sem.at[0])
            second = pltpu.make_async_copy(
                after_hbm, stale_ref.at[pl.ds(patch_rows, patch_rows)], copy_sem.at[1]
            )
            first.start()
            second.start()
            first.wait()
            second.wait()

    def compact(j, n):
        u = ids_ref[t, j]
        which = u // per_patch
        row = u - which * per_patch
        if stale_phase:
            keep = which != 1
            index = (which // 2) * per_patch + row
        else:
            keep = which == 1
            index = row

        @pl.when(keep)
        def _():
            list_ref[n] = index

        return n + keep.astype(jnp.int32)

    used = lax.fori_loop(0, count_ref[t], compact, jnp.int32(0))

    for h in range(local_heads):
        head = pl.ds(h * HEAD_DIM, HEAD_DIM)
        start_q = pl.multiple_of(t * TILE_TOKENS, TILE_TOKENS)
        query = fresh_ref[pl.ds(start_q, TILE_TOKENS), pl.ds(h * HEAD_DIM, HEAD_DIM)]
        if stale_phase:
            acc_ref[...] = acc_in[:, head]
            tot_ref[...] = tot_in[:, head]
            k_col, v_col = h * HEAD_DIM, width + h * HEAD_DIM
        else:
            acc_ref[:, head] = jnp.zeros((TILE_TOKENS, HEAD_DIM), jnp.float32)
            tot_ref[:, head] = jnp.zeros((TILE_TOKENS, HEAD_DIM), jnp.float32)
            k_col, v_col = width + h * HEAD_DIM, 2 * width + h * HEAD_DIM
        acc_at = slice(None) if stale_phase else head

        def accumulate(indices):
            starts = [pl.multiple_of(i * TILE_TOKENS, TILE_TOKENS) for i in indices]
            keys = jnp.concatenate(
                [keys_ref[pl.ds(a, TILE_TOKENS), pl.ds(k_col, HEAD_DIM)] for a in starts], axis=0
            )
            values = jnp.concatenate(
                [keys_ref[pl.ds(a, TILE_TOKENS), pl.ds(v_col, HEAD_DIM)] for a in starts], axis=0
            )
            scores = lax.dot_general(
                query, keys, (((1,), (1,)), ((), ())), preferred_element_type=jnp.float32
            )
            weight = jnp.exp2(jnp.tanh(scores * factor) * lift - lift)
            part = weight[:, 0:HEAD_DIM]
            for c in range(1, weight.shape[1] // HEAD_DIM):
                part = part + weight[:, c * HEAD_DIM:(c + 1) * HEAD_DIM]
            tot_ref[:, acc_at] += part
            acc_ref[:, acc_at] += jnp.dot(
                weight.astype(jnp.bfloat16), values, preferred_element_type=jnp.float32
            )

        def group(p, carry):
            accumulate([list_ref[SLOT_GROUP * p + i] for i in range(SLOT_GROUP)])
            return carry

        lax.fori_loop(0, used // SLOT_GROUP, group, 0)
        for left in range(1, SLOT_GROUP):

            @pl.when(used % SLOT_GROUP == left)
            def _():
                accumulate([list_ref[used - left + i] for i in range(left)])

        if stale_phase:
            total = jnp.sum(tot_ref[...], axis=1, keepdims=True)
            o_ref[:, head] = (acc_ref[...] / total).astype(o_ref.dtype)


def tile_attention(fresh, before, after, local_ids, tile_count, local_heads, per_patch):
    rows = fresh.shape[0]
    width = local_heads * HEAD_DIM
    tiles = rows // TILE_TOKENS

    def whole(array):
        return pl.BlockSpec(array.shape, lambda t, ids, cnt: (0, 0))

    tile = pl.BlockSpec((TILE_TOKENS, width), lambda t, ids, cnt: (t, 0))
    partial = jax.ShapeDtypeStruct((rows, width), jnp.float32)
    acc, tot = pl.pallas_call(
        functools.partial(attention_kernel, local_heads, per_patch, False),
        out_shape=(partial, partial),
        grid_spec=pltpu.PrefetchScalarGridSpec(
            num_scalar_prefetch=2,
            grid=(tiles,),
            in_specs=[whole(fresh)],
            out_specs=(tile, tile),
            scratch_shapes=[pltpu.SMEM((KEY_SLOTS,), jnp.int32)],
        ),
    )(local_ids, tile_count, fresh)
    hbm = pl.BlockSpec(memory_space=pl.ANY)
    return pl.pallas_call(
        functools.partial(attention_kernel, local_heads, per_patch, True),
        out_shape=jax.ShapeDtypeStruct((rows, width), jnp.bfloat16),
        grid_spec=pltpu.PrefetchScalarGridSpec(
            num_scalar_prefetch=2,
            grid=(tiles,),
            in_specs=[whole(fresh), hbm, hbm, tile, tile],
            out_specs=tile,
            scratch_shapes=[
                pltpu.VMEM((2 * rows, before.shape[1]), before.dtype),
                pltpu.SemaphoreType.DMA((2,)),
                pltpu.SMEM((KEY_SLOTS,), jnp.int32),
                pltpu.VMEM((TILE_TOKENS, HEAD_DIM), jnp.float32),
                pltpu.VMEM((TILE_TOKENS, HEAD_DIM), jnp.float32),
            ],
        ),
        compiler_params=pltpu.CompilerParams(dimension_semantics=("arbitrary",)),
    )(local_ids, tile_count, fresh, before, after, acc, tot)


def on_device(query, fresh_key, fresh_value, stale_key, stale_value, key_tiles, tile_count):
    seq_count = lax.axis_size("seq")
    local_heads = NUM_HEADS // seq_count
    width = local_heads * HEAD_DIM
    per_patch = TILES_H * TILES_W
    rows = query.shape[0]
    patch_rows = rows * seq_count

    def interleaved(arrays):
        parts = [a.reshape(rows, seq_count, width) for a in arrays]
        joined = jnp.concatenate(parts, axis=2).transpose(1, 0, 2)
        moved = lax.all_to_all(joined, "seq", split_axis=0, concat_axis=0, tiled=True)
        return moved.reshape(patch_rows, len(arrays) * width)

    stale = interleaved([stale_key, stale_value])
    framed = with_halo(stale, (("patch", 0),), patch_rows)
    before = framed[:patch_rows]
    after = framed[2 * patch_rows :]
    fresh = interleaved([query, fresh_key, fresh_value])
    first_tile = (lax.axis_index("patch") - 1) * per_patch
    local_ids = (key_tiles - first_tile).astype(jnp.int32)
    merged = tile_attention(
        fresh, before, after, local_ids, tile_count.astype(jnp.int32), local_heads, per_patch
    )
    return lax.all_to_all(merged, "seq", split_axis=0, concat_axis=1, tiled=True)


def solution(mesh):
    return jax.shard_map(
        on_device,
        mesh=mesh,
        in_specs=(
            P(("cfg", "patch", "seq"), None),
            P(("cfg", "patch", "seq"), None),
            P(("cfg", "patch", "seq"), None),
            P(("cfg", "patch", "seq"), None),
            P(("cfg", "patch", "seq"), None),
            P("patch", None),
            P("patch"),
        ),
        out_specs=P(("cfg", "patch", "seq"), None),
        check_vma=False,
    )
```

```python
import functools

import jax
import jax.numpy as jnp
from jax import lax
from jax.experimental import pallas as pl
from jax.experimental.pallas import tpu as pltpu
from jax.sharding import PartitionSpec as P

NUM_HEADS = 16
HEAD_DIM = 128
TILE_TOKENS = 384
TILES_H = 2
TILES_W = 3
KEY_SLOTS = 18
SLOT_GROUP = 3


soft_cap = 8.0


def with_halo(x, sides, width):
    for axis, dim in sides:
        size, length = (lax.axis_size(axis), x.shape[dim])
        up = [(i, (i + 1) % size) for i in range(size - 1)]
        down = [(j, i) for i, j in up]
        last = lax.slice_in_dim(x, length - width, length, axis=dim)
        leading = lax.slice_in_dim(x, 0, width, axis=dim)
        before = lax.ppermute(last, axis, up)
        after = lax.ppermute(leading, axis, down)
        x = jnp.concatenate([before, x, after], axis=dim)
    return x


def attention_kernel(local_heads, per_patch, stale_phase, ids_ref, count_ref, fresh_ref, *refs):
    if stale_phase:
        before_in, after_in, acc_in, tot_in, o_ref, keys_ref, copy_sem, list_ref, acc_ref, tot_ref = refs
    else:
        acc_ref, tot_ref, list_ref = refs
        keys_ref = fresh_ref
    t = pl.program_id(0)
    width = local_heads * HEAD_DIM
    patch_rows = fresh_ref.shape[0]
    factor = 1.0 / (HEAD_DIM**0.5) / soft_cap
    lift = soft_cap * 1.4426950408889634

    if stale_phase:

        @pl.when(t == 0)
        def _():
            copies = [
                pltpu.make_async_copy(before_in, keys_ref.at[pl.ds(0, patch_rows)], copy_sem.at[0]),
                pltpu.make_async_copy(
                    fresh_ref.at[:, pl.ds(width, 2 * width)],
                    keys_ref.at[pl.ds(patch_rows, patch_rows)],
                    copy_sem.at[1],
                ),
                pltpu.make_async_copy(
                    after_in, keys_ref.at[pl.ds(2 * patch_rows, patch_rows)], copy_sem.at[2]
                ),
            ]
            for c in copies:
                c.start()
            for c in copies:
                c.wait()

    def own(j):
        return ids_ref[t, j] // per_patch == 1

    own_count = lax.fori_loop(0, count_ref[t], lambda j, n: n + own(j).astype(jnp.int32), jnp.int32(0))
    first_pass = own_count - own_count % SLOT_GROUP

    def compact(j, carry):
        n, seen = carry
        u = ids_ref[t, j]
        mine = own(j)
        early = jnp.logical_and(mine, seen < first_pass)
        if stale_phase:
            keep = jnp.logical_not(early)
            index = u
        else:
            keep = early
            index = u - per_patch

        @pl.when(keep)
        def _():
            list_ref[n] = index

        return n + keep.astype(jnp.int32), seen + mine.astype(jnp.int32)

    used, _ = lax.fori_loop(0, count_ref[t], compact, (jnp.int32(0), jnp.int32(0)))

    for h in range(local_heads):
        head = pl.ds(h * HEAD_DIM, HEAD_DIM)
        start_q = pl.multiple_of(t * TILE_TOKENS, TILE_TOKENS)
        query = fresh_ref[pl.ds(start_q, TILE_TOKENS), pl.ds(h * HEAD_DIM, HEAD_DIM)]
        if stale_phase:
            acc_ref[...] = acc_in[:, head]
            tot_ref[...] = tot_in[:, head]
            k_col, v_col = h * HEAD_DIM, width + h * HEAD_DIM
        else:
            acc_ref[:, head] = jnp.zeros((TILE_TOKENS, HEAD_DIM), jnp.float32)
            tot_ref[:, head] = jnp.zeros((TILE_TOKENS, HEAD_DIM), jnp.float32)
            k_col, v_col = width + h * HEAD_DIM, 2 * width + h * HEAD_DIM
        acc_at = slice(None) if stale_phase else head

        def weights(index):
            start = pl.multiple_of(index * TILE_TOKENS, TILE_TOKENS)
            keys = keys_ref[pl.ds(start, TILE_TOKENS), pl.ds(k_col, HEAD_DIM)]
            values = keys_ref[pl.ds(start, TILE_TOKENS), pl.ds(v_col, HEAD_DIM)]
            scores = lax.dot_general(
                query, keys, (((1,), (1,)), ((), ())), preferred_element_type=jnp.float32
            )
            weight = jnp.exp2(jnp.tanh(scores * factor) * lift - lift)
            part = weight[:, 0:HEAD_DIM]
            for c in range(1, TILE_TOKENS // HEAD_DIM):
                part = part + weight[:, c * HEAD_DIM:(c + 1) * HEAD_DIM]
            return weight.astype(jnp.bfloat16), part, values

        def accumulate(indices):
            got = [weights(i) for i in indices]
            part = got[0][1]
            for g in got[1:]:
                part = part + g[1]
            tot_ref[:, acc_at] += part
            acc_ref[:, acc_at] += jnp.dot(
                jnp.concatenate([g[0] for g in got], axis=1),
                jnp.concatenate([g[2] for g in got], axis=0),
                preferred_element_type=jnp.float32,
            )

        def group(p, carry):
            accumulate([list_ref[SLOT_GROUP * p + i] for i in range(SLOT_GROUP)])
            return carry

        lax.fori_loop(0, used // SLOT_GROUP, group, 0)
        if stale_phase:
            for left in range(1, SLOT_GROUP):

                @pl.when(used % SLOT_GROUP == left)
                def _():
                    accumulate([list_ref[used - left + i] for i in range(left)])

            total = jnp.sum(tot_ref[...], axis=1, keepdims=True)
            o_ref[:, head] = (acc_ref[...] / total).astype(o_ref.dtype)


def tile_attention(fresh, before, after, local_ids, tile_count, local_heads, per_patch):
    rows = fresh.shape[0]
    width = local_heads * HEAD_DIM
    tiles = rows // TILE_TOKENS

    def whole(array):
        return pl.BlockSpec(array.shape, lambda t, ids, cnt: (0, 0))

    tile = pl.BlockSpec((TILE_TOKENS, width), lambda t, ids, cnt: (t, 0))
    partial = jax.ShapeDtypeStruct((rows, width), jnp.float32)
    acc, tot = pl.pallas_call(
        functools.partial(attention_kernel, local_heads, per_patch, False),
        out_shape=(partial, partial),
        grid_spec=pltpu.PrefetchScalarGridSpec(
            num_scalar_prefetch=2,
            grid=(tiles,),
            in_specs=[whole(fresh)],
            out_specs=(tile, tile),
            scratch_shapes=[pltpu.SMEM((KEY_SLOTS,), jnp.int32)],
        ),
    )(local_ids, tile_count, fresh)
    return pl.pallas_call(
        functools.partial(attention_kernel, local_heads, per_patch, True),
        out_shape=jax.ShapeDtypeStruct((rows, width), jnp.bfloat16),
        grid_spec=pltpu.PrefetchScalarGridSpec(
            num_scalar_prefetch=2,
            grid=(tiles,),
            in_specs=[whole(fresh), whole(before), whole(after), tile, tile],
            out_specs=tile,
            scratch_shapes=[
                pltpu.VMEM((3 * rows, before.shape[1]), before.dtype),
                pltpu.SemaphoreType.DMA((3,)),
                pltpu.SMEM((KEY_SLOTS,), jnp.int32),
                pltpu.VMEM((TILE_TOKENS, HEAD_DIM), jnp.float32),
                pltpu.VMEM((TILE_TOKENS, HEAD_DIM), jnp.float32),
            ],
        ),
        compiler_params=pltpu.CompilerParams(dimension_semantics=("arbitrary",)),
    )(local_ids, tile_count, fresh, before, after, acc, tot)


def on_device(query, fresh_key, fresh_value, stale_key, stale_value, key_tiles, tile_count):
    seq_count = lax.axis_size("seq")
    local_heads = NUM_HEADS // seq_count
    width = local_heads * HEAD_DIM
    per_patch = TILES_H * TILES_W
    rows = query.shape[0]
    patch_rows = rows * seq_count

    def interleaved(arrays):
        parts = [a.reshape(rows, seq_count, width) for a in arrays]
        joined = jnp.concatenate(parts, axis=2).transpose(1, 0, 2)
        moved = lax.all_to_all(joined, "seq", split_axis=0, concat_axis=0, tiled=True)
        return moved.reshape(patch_rows, len(arrays) * width)

    stale = interleaved([stale_key, stale_value])
    framed = with_halo(stale, (("patch", 0),), patch_rows)
    before = framed[:patch_rows]
    after = framed[2 * patch_rows :]
    fresh = interleaved([query, fresh_key, fresh_value])
    first_tile = (lax.axis_index("patch") - 1) * per_patch
    local_ids = (key_tiles - first_tile).astype(jnp.int32)
    merged = tile_attention(
        fresh, before, after, local_ids, tile_count.astype(jnp.int32), local_heads, per_patch
    )
    return lax.all_to_all(merged, "seq", split_axis=0, concat_axis=1, tiled=True)


def solution(mesh):
    return jax.shard_map(
        on_device,
        mesh=mesh,
        in_specs=(
            P(("cfg", "patch", "seq"), None),
            P(("cfg", "patch", "seq"), None),
            P(("cfg", "patch", "seq"), None),
            P(("cfg", "patch", "seq"), None),
            P(("cfg", "patch", "seq"), None),
            P("patch", None),
            P("patch"),
        ),
        out_specs=P(("cfg", "patch", "seq"), None),
        check_vma=False,
    )
```

```python
import functools

import jax
import jax.numpy as jnp
from jax import lax
from jax.experimental import pallas as pl
from jax.experimental.pallas import tpu as pltpu
from jax.sharding import PartitionSpec as P

NUM_HEADS = 16
HEAD_DIM = 128
TILE_TOKENS = 384
TILES_H = 2
TILES_W = 3
KEY_SLOTS = 18
SLOT_GROUP = 3


soft_cap = 8.0


def with_halo(x, sides, width):
    for axis, dim in sides:
        size, length = (lax.axis_size(axis), x.shape[dim])
        up = [(i, (i + 1) % size) for i in range(size - 1)]
        down = [(j, i) for i, j in up]
        last = lax.slice_in_dim(x, length - width, length, axis=dim)
        leading = lax.slice_in_dim(x, 0, width, axis=dim)
        before = lax.ppermute(last, axis, up)
        after = lax.ppermute(leading, axis, down)
        x = jnp.concatenate([before, x, after], axis=dim)
    return x


def attention_kernel(local_heads, per_patch, stale_phase, ids_ref, count_ref, fresh_ref, *refs):
    if stale_phase:
        before_hbm, after_hbm, acc_in, tot_in, o_ref, stale_ref, copy_sem, list_ref, acc_ref, tot_ref = refs
        keys_ref = stale_ref
    else:
        acc_ref, tot_ref, list_ref = refs
        keys_ref = fresh_ref
    t = pl.program_id(0)
    width = local_heads * HEAD_DIM
    patch_rows = fresh_ref.shape[0]
    factor = 1.0 / (HEAD_DIM**0.5) / soft_cap
    lift = soft_cap * 1.4426950408889634

    if stale_phase:

        @pl.when(t == 0)
        def _():
            first = pltpu.make_async_copy(before_hbm, stale_ref.at[pl.ds(0, patch_rows)], copy_sem.at[0])
            second = pltpu.make_async_copy(
                after_hbm, stale_ref.at[pl.ds(patch_rows, patch_rows)], copy_sem.at[1]
            )
            first.start()
            second.start()
            first.wait()
            second.wait()

    def compact(j, n):
        u = ids_ref[t, j]
        which = u // per_patch
        row = u - which * per_patch
        if stale_phase:
            keep = which != 1
            index = (which // 2) * per_patch + row
        else:
            keep = which == 1
            index = row

        @pl.when(keep)
        def _():
            list_ref[n] = index

        return n + keep.astype(jnp.int32)

    used = lax.fori_loop(0, count_ref[t], compact, jnp.int32(0))

    for h in range(local_heads):
        head = pl.ds(h * HEAD_DIM, HEAD_DIM)
        start_q = pl.multiple_of(t * TILE_TOKENS, TILE_TOKENS)
        query = fresh_ref[pl.ds(start_q, TILE_TOKENS), pl.ds(h * HEAD_DIM, HEAD_DIM)]
        if stale_phase:
            acc_ref[...] = acc_in[:, head]
            tot_ref[...] = tot_in[:, head]
            k_col, v_col = h * HEAD_DIM, width + h * HEAD_DIM
        else:
            acc_ref[:, head] = jnp.zeros((TILE_TOKENS, HEAD_DIM), jnp.float32)
            tot_ref[:, head] = jnp.zeros((TILE_TOKENS, HEAD_DIM), jnp.float32)
            k_col, v_col = width + h * HEAD_DIM, 2 * width + h * HEAD_DIM
        acc_at = slice(None) if stale_phase else head

        def weights(index):
            start = pl.multiple_of(index * TILE_TOKENS, TILE_TOKENS)
            keys = keys_ref[pl.ds(start, TILE_TOKENS), pl.ds(k_col, HEAD_DIM)]
            values = keys_ref[pl.ds(start, TILE_TOKENS), pl.ds(v_col, HEAD_DIM)]
            scores = lax.dot_general(
                query, keys, (((1,), (1,)), ((), ())), preferred_element_type=jnp.float32
            )
            weight = jnp.exp2(jnp.tanh(scores * factor) * lift - lift)
            part = weight[:, 0:HEAD_DIM]
            for c in range(1, TILE_TOKENS // HEAD_DIM):
                part = part + weight[:, c * HEAD_DIM:(c + 1) * HEAD_DIM]
            return weight.astype(jnp.bfloat16), part, values

        def accumulate(indices):
            got = [weights(i) for i in indices]
            part = got[0][1]
            for g in got[1:]:
                part = part + g[1]
            tot_ref[:, acc_at] += part
            acc_ref[:, acc_at] += jnp.dot(
                jnp.concatenate([g[0] for g in got], axis=1),
                jnp.concatenate([g[2] for g in got], axis=0),
                preferred_element_type=jnp.float32,
            )

        def group(p, carry):
            accumulate([list_ref[SLOT_GROUP * p + i] for i in range(SLOT_GROUP)])
            return carry

        lax.fori_loop(0, used // SLOT_GROUP, group, 0)
        for left in range(1, SLOT_GROUP):

            @pl.when(used % SLOT_GROUP == left)
            def _():
                accumulate([list_ref[used - left + i] for i in range(left)])

        if stale_phase:
            total = jnp.sum(tot_ref[...], axis=1, keepdims=True)
            o_ref[:, head] = (acc_ref[...] / total).astype(o_ref.dtype)


def tile_attention(fresh, before, after, local_ids, tile_count, local_heads, per_patch):
    rows = fresh.shape[0]
    width = local_heads * HEAD_DIM
    tiles = rows // TILE_TOKENS

    def whole(array):
        return pl.BlockSpec(array.shape, lambda t, ids, cnt: (0, 0))

    tile = pl.BlockSpec((TILE_TOKENS, width), lambda t, ids, cnt: (t, 0))
    partial = jax.ShapeDtypeStruct((rows, width), jnp.float32)
    acc, tot = pl.pallas_call(
        functools.partial(attention_kernel, local_heads, per_patch, False),
        out_shape=(partial, partial),
        grid_spec=pltpu.PrefetchScalarGridSpec(
            num_scalar_prefetch=2,
            grid=(tiles,),
            in_specs=[whole(fresh)],
            out_specs=(tile, tile),
            scratch_shapes=[pltpu.SMEM((KEY_SLOTS,), jnp.int32)],
        ),
    )(local_ids, tile_count, fresh)
    hbm = pl.BlockSpec(memory_space=pl.ANY)
    return pl.pallas_call(
        functools.partial(attention_kernel, local_heads, per_patch, True),
        out_shape=jax.ShapeDtypeStruct((rows, width), jnp.bfloat16),
        grid_spec=pltpu.PrefetchScalarGridSpec(
            num_scalar_prefetch=2,
            grid=(tiles,),
            in_specs=[whole(fresh), hbm, hbm, tile, tile],
            out_specs=tile,
            scratch_shapes=[
                pltpu.VMEM((2 * rows, before.shape[1]), before.dtype),
                pltpu.SemaphoreType.DMA((2,)),
                pltpu.SMEM((KEY_SLOTS,), jnp.int32),
                pltpu.VMEM((TILE_TOKENS, HEAD_DIM), jnp.float32),
                pltpu.VMEM((TILE_TOKENS, HEAD_DIM), jnp.float32),
            ],
        ),
        compiler_params=pltpu.CompilerParams(dimension_semantics=("arbitrary",)),
    )(local_ids, tile_count, fresh, before, after, acc, tot)


def regroup_kernel(width, *refs):
    *in_refs, o_ref = refs
    seq_count = o_ref.shape[0]
    for d in range(seq_count):
        for a, ref in enumerate(in_refs):
            o_ref[d, :, a * width:(a + 1) * width] = ref[:, d * width:(d + 1) * width]


def regroup(arrays, seq_count, width):
    rows = arrays[0].shape[0]
    return pl.pallas_call(
        functools.partial(regroup_kernel, width),
        out_shape=jax.ShapeDtypeStruct((seq_count, rows, len(arrays) * width), arrays[0].dtype),
    )(*arrays)


def on_device(query, fresh_key, fresh_value, stale_key, stale_value, key_tiles, tile_count):
    seq_count = lax.axis_size("seq")
    local_heads = NUM_HEADS // seq_count
    width = local_heads * HEAD_DIM
    per_patch = TILES_H * TILES_W
    rows = query.shape[0]
    patch_rows = rows * seq_count

    def interleaved(arrays):
        parts = [a.reshape(rows, seq_count, width) for a in arrays]
        joined = jnp.concatenate(parts, axis=2).transpose(1, 0, 2)
        moved = lax.all_to_all(joined, "seq", split_axis=0, concat_axis=0, tiled=True)
        return moved.reshape(patch_rows, len(arrays) * width)

    joined = regroup([stale_key, stale_value], seq_count, width)
    stale = lax.all_to_all(joined, "seq", split_axis=0, concat_axis=0, tiled=True)
    stale = stale.reshape(patch_rows, 2 * width)
    framed = with_halo(stale, (("patch", 0),), patch_rows)
    before = framed[:patch_rows]
    after = framed[2 * patch_rows :]
    fresh = interleaved([query, fresh_key, fresh_value])
    first_tile = (lax.axis_index("patch") - 1) * per_patch
    local_ids = (key_tiles - first_tile).astype(jnp.int32)
    merged = tile_attention(
        fresh, before, after, local_ids, tile_count.astype(jnp.int32), local_heads, per_patch
    )
    return lax.all_to_all(merged, "seq", split_axis=0, concat_axis=1, tiled=True)


def solution(mesh):
    return jax.shard_map(
        on_device,
        mesh=mesh,
        in_specs=(
            P(("cfg", "patch", "seq"), None),
            P(("cfg", "patch", "seq"), None),
            P(("cfg", "patch", "seq"), None),
            P(("cfg", "patch", "seq"), None),
            P(("cfg", "patch", "seq"), None),
            P("patch", None),
            P("patch"),
        ),
        out_specs=P(("cfg", "patch", "seq"), None),
        check_vma=False,
    )
```

```python
import functools

import jax
import jax.numpy as jnp
from jax import lax
from jax.experimental import pallas as pl
from jax.experimental.pallas import tpu as pltpu
from jax.sharding import PartitionSpec as P

NUM_HEADS = 16
HEAD_DIM = 128
TILE_TOKENS = 384
TILES_H = 2
TILES_W = 3
KEY_SLOTS = 18
SLOT_GROUP = 3


soft_cap = 8.0


def with_halo(x, sides, width):
    for axis, dim in sides:
        size, length = (lax.axis_size(axis), x.shape[dim])
        up = [(i, (i + 1) % size) for i in range(size - 1)]
        down = [(j, i) for i, j in up]
        last = lax.slice_in_dim(x, length - width, length, axis=dim)
        leading = lax.slice_in_dim(x, 0, width, axis=dim)
        before = lax.ppermute(last, axis, up)
        after = lax.ppermute(leading, axis, down)
        x = jnp.concatenate([before, x, after], axis=dim)
    return x


def attention_kernel(local_heads, per_patch, stale_phase, ids_ref, count_ref, fresh_ref, *refs):
    if stale_phase:
        before_hbm, after_hbm, acc_in, tot_in, o_ref, stale_ref, copy_sem, list_ref, acc_ref, tot_ref = refs
        keys_ref = stale_ref
    else:
        acc_ref, tot_ref, list_ref = refs
        keys_ref = fresh_ref
    t = pl.program_id(0)
    width = local_heads * HEAD_DIM
    patch_rows = fresh_ref.shape[0]
    factor = 1.0 / (HEAD_DIM**0.5) / soft_cap
    lift = soft_cap * 1.4426950408889634

    if stale_phase:

        @pl.when(t == 0)
        def _():
            first = pltpu.make_async_copy(before_hbm, stale_ref.at[pl.ds(0, patch_rows)], copy_sem.at[0])
            second = pltpu.make_async_copy(
                after_hbm, stale_ref.at[pl.ds(patch_rows, patch_rows)], copy_sem.at[1]
            )
            first.start()
            second.start()
            first.wait()
            second.wait()

    def compact(j, n):
        u = ids_ref[t, j]
        which = u // per_patch
        row = u - which * per_patch
        if stale_phase:
            keep = which != 1
            index = (which // 2) * per_patch + row
        else:
            keep = which == 1
            index = row

        @pl.when(keep)
        def _():
            list_ref[n] = index

        return n + keep.astype(jnp.int32)

    used = lax.fori_loop(0, count_ref[t], compact, jnp.int32(0))

    for h in range(local_heads):
        head = pl.ds(h * HEAD_DIM, HEAD_DIM)
        start_q = pl.multiple_of(t * TILE_TOKENS, TILE_TOKENS)
        query = fresh_ref[pl.ds(start_q, TILE_TOKENS), pl.ds(h * HEAD_DIM, HEAD_DIM)]
        if stale_phase:
            acc_ref[...] = acc_in[:, head]
            tot_ref[...] = tot_in[:, head]
            k_col, v_col = h * HEAD_DIM, width + h * HEAD_DIM
        else:
            acc_ref[:, head] = jnp.zeros((TILE_TOKENS, HEAD_DIM), jnp.float32)
            tot_ref[:, head] = jnp.zeros((TILE_TOKENS, HEAD_DIM), jnp.float32)
            k_col, v_col = width + h * HEAD_DIM, 2 * width + h * HEAD_DIM
        acc_at = slice(None) if stale_phase else head

        def weights(index):
            start = pl.multiple_of(index * TILE_TOKENS, TILE_TOKENS)
            keys = keys_ref[pl.ds(start, TILE_TOKENS), pl.ds(k_col, HEAD_DIM)]
            values = keys_ref[pl.ds(start, TILE_TOKENS), pl.ds(v_col, HEAD_DIM)]
            scores = lax.dot_general(
                query, keys, (((1,), (1,)), ((), ())), preferred_element_type=jnp.float32
            )
            weight = jnp.exp2(jnp.tanh(scores * factor) * lift - lift)
            part = weight[:, 0:HEAD_DIM]
            for c in range(1, TILE_TOKENS // HEAD_DIM):
                part = part + weight[:, c * HEAD_DIM:(c + 1) * HEAD_DIM]
            return weight.astype(jnp.bfloat16), part, values

        def accumulate(indices):
            got = [weights(i) for i in indices]
            part = got[0][1]
            for g in got[1:]:
                part = part + g[1]
            tot_ref[:, acc_at] += part
            acc_ref[:, acc_at] += jnp.dot(
                jnp.concatenate([g[0] for g in got], axis=1),
                jnp.concatenate([g[2] for g in got], axis=0),
                preferred_element_type=jnp.float32,
            )

        def group(p, carry):
            accumulate([list_ref[SLOT_GROUP * p + i] for i in range(SLOT_GROUP)])
            return carry

        lax.fori_loop(0, used // SLOT_GROUP, group, 0)
        for left in range(1, SLOT_GROUP):

            @pl.when(used % SLOT_GROUP == left)
            def _():
                accumulate([list_ref[used - left + i] for i in range(left)])

        if stale_phase:
            total = jnp.sum(tot_ref[...], axis=1, keepdims=True)
            o_ref[:, head] = (acc_ref[...] / total).astype(o_ref.dtype)


def tile_attention(fresh, before, after, local_ids, tile_count, local_heads, per_patch):
    rows = fresh.shape[0]
    width = local_heads * HEAD_DIM
    tiles = rows // TILE_TOKENS

    def whole(array):
        return pl.BlockSpec(array.shape, lambda t, ids, cnt: (0, 0))

    fresh = pltpu.with_memory_space_constraint(fresh, pltpu.VMEM)
    resident = pl.BlockSpec(memory_space=pltpu.VMEM)

    tile = pl.BlockSpec((TILE_TOKENS, width), lambda t, ids, cnt: (t, 0))
    partial = jax.ShapeDtypeStruct((rows, width), jnp.float32)
    acc, tot = pl.pallas_call(
        functools.partial(attention_kernel, local_heads, per_patch, False),
        out_shape=(partial, partial),
        grid_spec=pltpu.PrefetchScalarGridSpec(
            num_scalar_prefetch=2,
            grid=(tiles,),
            in_specs=[resident],
            out_specs=(tile, tile),
            scratch_shapes=[pltpu.SMEM((KEY_SLOTS,), jnp.int32)],
        ),
    )(local_ids, tile_count, fresh)
    hbm = pl.BlockSpec(memory_space=pl.ANY)
    return pl.pallas_call(
        functools.partial(attention_kernel, local_heads, per_patch, True),
        out_shape=jax.ShapeDtypeStruct((rows, width), jnp.bfloat16),
        grid_spec=pltpu.PrefetchScalarGridSpec(
            num_scalar_prefetch=2,
            grid=(tiles,),
            in_specs=[resident, hbm, hbm, tile, tile],
            out_specs=tile,
            scratch_shapes=[
                pltpu.VMEM((2 * rows, before.shape[1]), before.dtype),
                pltpu.SemaphoreType.DMA((2,)),
                pltpu.SMEM((KEY_SLOTS,), jnp.int32),
                pltpu.VMEM((TILE_TOKENS, HEAD_DIM), jnp.float32),
                pltpu.VMEM((TILE_TOKENS, HEAD_DIM), jnp.float32),
            ],
        ),
        compiler_params=pltpu.CompilerParams(dimension_semantics=("arbitrary",)),
    )(local_ids, tile_count, fresh, before, after, acc, tot)


def regroup_kernel(width, *refs):
    *in_refs, o_ref = refs
    seq_count = o_ref.shape[0]
    for d in range(seq_count):
        for a, ref in enumerate(in_refs):
            o_ref[d, :, a * width:(a + 1) * width] = ref[:, d * width:(d + 1) * width]


def regroup(arrays, seq_count, width):
    rows = arrays[0].shape[0]
    return pl.pallas_call(
        functools.partial(regroup_kernel, width),
        out_shape=jax.ShapeDtypeStruct((seq_count, rows, len(arrays) * width), arrays[0].dtype),
    )(*arrays)


def on_device(query, fresh_key, fresh_value, stale_key, stale_value, key_tiles, tile_count):
    seq_count = lax.axis_size("seq")
    local_heads = NUM_HEADS // seq_count
    width = local_heads * HEAD_DIM
    per_patch = TILES_H * TILES_W
    rows = query.shape[0]
    patch_rows = rows * seq_count

    def interleaved(arrays):
        parts = [a.reshape(rows, seq_count, width) for a in arrays]
        joined = jnp.concatenate(parts, axis=2).transpose(1, 0, 2)
        moved = lax.all_to_all(joined, "seq", split_axis=0, concat_axis=0, tiled=True)
        return moved.reshape(patch_rows, len(arrays) * width)

    joined = regroup([stale_key, stale_value], seq_count, width)
    stale = lax.all_to_all(joined, "seq", split_axis=0, concat_axis=0, tiled=True)
    stale = stale.reshape(patch_rows, 2 * width)
    framed = with_halo(stale, (("patch", 0),), patch_rows)
    before = framed[:patch_rows]
    after = framed[2 * patch_rows :]
    fresh = interleaved([query, fresh_key, fresh_value])
    first_tile = (lax.axis_index("patch") - 1) * per_patch
    local_ids = (key_tiles - first_tile).astype(jnp.int32)
    merged = tile_attention(
        fresh, before, after, local_ids, tile_count.astype(jnp.int32), local_heads, per_patch
    )
    return lax.all_to_all(merged, "seq", split_axis=0, concat_axis=1, tiled=True)


def solution(mesh):
    return jax.shard_map(
        on_device,
        mesh=mesh,
        in_specs=(
            P(("cfg", "patch", "seq"), None),
            P(("cfg", "patch", "seq"), None),
            P(("cfg", "patch", "seq"), None),
            P(("cfg", "patch", "seq"), None),
            P(("cfg", "patch", "seq"), None),
            P("patch", None),
            P("patch"),
        ),
        out_specs=P(("cfg", "patch", "seq"), None),
        check_vma=False,
    )
```

```python
import functools

import jax
import jax.numpy as jnp
from jax import lax
from jax.experimental import pallas as pl
from jax.experimental.pallas import tpu as pltpu
from jax.sharding import PartitionSpec as P

NUM_HEADS = 16
HEAD_DIM = 128
TILE_TOKENS = 384
TILES_H = 2
TILES_W = 3
KEY_SLOTS = 18
SLOT_GROUP = 3


soft_cap = 8.0


def with_halo(x, sides, width):
    for axis, dim in sides:
        size, length = (lax.axis_size(axis), x.shape[dim])
        up = [(i, (i + 1) % size) for i in range(size - 1)]
        down = [(j, i) for i, j in up]
        last = lax.slice_in_dim(x, length - width, length, axis=dim)
        leading = lax.slice_in_dim(x, 0, width, axis=dim)
        before = lax.ppermute(last, axis, up)
        after = lax.ppermute(leading, axis, down)
        x = jnp.concatenate([before, x, after], axis=dim)
    return x


def attention_kernel(local_heads, per_patch, stale_phase, ids_ref, count_ref, fresh_ref, *refs):
    if stale_phase:
        before_hbm, after_hbm, acc_in, tot_in, o_ref, stale_ref, copy_sem, list_ref, acc_ref, tot_ref = refs
        keys_ref = stale_ref
    else:
        acc_ref, tot_ref, list_ref = refs
        keys_ref = fresh_ref
    t = pl.program_id(0)
    width = local_heads * HEAD_DIM
    patch_rows = fresh_ref.shape[0]
    factor = 1.0 / (HEAD_DIM**0.5) / soft_cap
    lift = soft_cap * 1.4426950408889634

    if stale_phase:

        @pl.when(t == 0)
        def _():
            first = pltpu.make_async_copy(before_hbm, stale_ref.at[pl.ds(0, patch_rows)], copy_sem.at[0])
            second = pltpu.make_async_copy(
                after_hbm, stale_ref.at[pl.ds(patch_rows, patch_rows)], copy_sem.at[1]
            )
            first.start()
            second.start()
            first.wait()
            second.wait()

    def compact(j, n):
        u = ids_ref[t, j]
        which = u // per_patch
        row = u - which * per_patch
        if stale_phase:
            keep = which != 1
            index = (which // 2) * per_patch + row
        else:
            keep = which == 1
            index = row

        @pl.when(keep)
        def _():
            list_ref[n] = index

        return n + keep.astype(jnp.int32)

    used = lax.fori_loop(0, count_ref[t], compact, jnp.int32(0))

    for h in range(local_heads):
        head = pl.ds(h * HEAD_DIM, HEAD_DIM)
        start_q = pl.multiple_of(t * TILE_TOKENS, TILE_TOKENS)
        query = fresh_ref[pl.ds(start_q, TILE_TOKENS), pl.ds(h * HEAD_DIM, HEAD_DIM)]
        if stale_phase:
            acc_ref[...] = acc_in[:, head]
            tot_ref[...] = tot_in[:, head]
            k_col, v_col = h * HEAD_DIM, width + h * HEAD_DIM
        else:
            acc_ref[:, head] = jnp.zeros((TILE_TOKENS, HEAD_DIM), jnp.float32)
            tot_ref[:, head] = jnp.zeros((TILE_TOKENS, HEAD_DIM), jnp.float32)
            k_col, v_col = width + h * HEAD_DIM, 2 * width + h * HEAD_DIM
        acc_at = slice(None) if stale_phase else head

        def weights(index):
            start = pl.multiple_of(index * TILE_TOKENS, TILE_TOKENS)
            keys = keys_ref[pl.ds(start, TILE_TOKENS), pl.ds(k_col, HEAD_DIM)]
            values = keys_ref[pl.ds(start, TILE_TOKENS), pl.ds(v_col, HEAD_DIM)]
            scores = lax.dot_general(
                query, keys, (((1,), (1,)), ((), ())), preferred_element_type=jnp.float32
            )
            weight = jnp.exp2(jnp.tanh(scores * factor) * lift - lift)
            part = weight[:, 0:HEAD_DIM]
            for c in range(1, TILE_TOKENS // HEAD_DIM):
                part = part + weight[:, c * HEAD_DIM:(c + 1) * HEAD_DIM]
            return weight.astype(jnp.bfloat16), part, values

        def accumulate(indices):
            got = [weights(i) for i in indices]
            part = got[0][1]
            for g in got[1:]:
                part = part + g[1]
            tot_ref[:, acc_at] += part
            acc_ref[:, acc_at] += jnp.dot(
                jnp.concatenate([g[0] for g in got], axis=1),
                jnp.concatenate([g[2] for g in got], axis=0),
                preferred_element_type=jnp.float32,
            )

        def group(p, carry):
            accumulate([list_ref[SLOT_GROUP * p + i] for i in range(SLOT_GROUP)])
            return carry

        lax.fori_loop(0, used // SLOT_GROUP, group, 0)
        for left in range(1, SLOT_GROUP):

            @pl.when(used % SLOT_GROUP == left)
            def _():
                accumulate([list_ref[used - left + i] for i in range(left)])

        if stale_phase:
            total = jnp.sum(tot_ref[...], axis=1, keepdims=True)
            o_ref[:, head] = (acc_ref[...] / total).astype(o_ref.dtype)


def tile_attention(fresh, before, after, local_ids, tile_count, local_heads, per_patch):
    rows = fresh.shape[0]
    width = local_heads * HEAD_DIM
    tiles = rows // TILE_TOKENS

    def whole(array):
        return pl.BlockSpec(array.shape, lambda t, ids, cnt: (0, 0))

    fresh = pltpu.with_memory_space_constraint(fresh, pltpu.VMEM)
    resident = pl.BlockSpec(memory_space=pltpu.VMEM)

    tile = pl.BlockSpec((TILE_TOKENS, width), lambda t, ids, cnt: (t, 0))
    partial = jax.ShapeDtypeStruct((rows, width), jnp.float32)
    acc, tot = pl.pallas_call(
        functools.partial(attention_kernel, local_heads, per_patch, False),
        out_shape=(partial, partial),
        grid_spec=pltpu.PrefetchScalarGridSpec(
            num_scalar_prefetch=2,
            grid=(tiles,),
            in_specs=[resident],
            out_specs=(tile, tile),
            scratch_shapes=[pltpu.SMEM((KEY_SLOTS,), jnp.int32)],
        ),
    )(local_ids, tile_count, fresh)
    hbm = pl.BlockSpec(memory_space=pl.ANY)
    return pl.pallas_call(
        functools.partial(attention_kernel, local_heads, per_patch, True),
        out_shape=jax.ShapeDtypeStruct((rows, width), jnp.bfloat16),
        grid_spec=pltpu.PrefetchScalarGridSpec(
            num_scalar_prefetch=2,
            grid=(tiles,),
            in_specs=[resident, hbm, hbm, tile, tile],
            out_specs=tile,
            scratch_shapes=[
                pltpu.VMEM((2 * rows, before.shape[1]), before.dtype),
                pltpu.SemaphoreType.DMA((2,)),
                pltpu.SMEM((KEY_SLOTS,), jnp.int32),
                pltpu.VMEM((TILE_TOKENS, HEAD_DIM), jnp.float32),
                pltpu.VMEM((TILE_TOKENS, HEAD_DIM), jnp.float32),
            ],
        ),
        compiler_params=pltpu.CompilerParams(dimension_semantics=("arbitrary",)),
    )(local_ids, tile_count, fresh, before, after, acc, tot)


def regroup_kernel(width, *refs):
    *in_refs, o_ref = refs
    for d in range(o_ref.shape[0]):
        for a, ref in enumerate(in_refs):
            o_ref[d, :, a * width:(a + 1) * width] = ref[:, d * width:(d + 1) * width]


def regroup(arrays, seq_count, width, steps=4):
    rows = arrays[0].shape[0]
    per_step = seq_count // steps
    return pl.pallas_call(
        functools.partial(regroup_kernel, width),
        out_shape=jax.ShapeDtypeStruct((seq_count, rows, len(arrays) * width), arrays[0].dtype),
        grid=(steps,),
        in_specs=[pl.BlockSpec((rows, per_step * width), lambda i: (0, i))] * len(arrays),
        out_specs=pl.BlockSpec((per_step, rows, len(arrays) * width), lambda i: (i, 0, 0)),
    )(*arrays)


def on_device(query, fresh_key, fresh_value, stale_key, stale_value, key_tiles, tile_count):
    seq_count = lax.axis_size("seq")
    local_heads = NUM_HEADS // seq_count
    width = local_heads * HEAD_DIM
    per_patch = TILES_H * TILES_W
    rows = query.shape[0]
    patch_rows = rows * seq_count

    def interleaved(arrays):
        parts = [a.reshape(rows, seq_count, width) for a in arrays]
        joined = jnp.concatenate(parts, axis=2).transpose(1, 0, 2)
        moved = lax.all_to_all(joined, "seq", split_axis=0, concat_axis=0, tiled=True)
        return moved.reshape(patch_rows, len(arrays) * width)

    joined = regroup([stale_key, stale_value], seq_count, width)
    stale = lax.all_to_all(joined, "seq", split_axis=0, concat_axis=0, tiled=True)
    stale = stale.reshape(patch_rows, 2 * width)
    framed = with_halo(stale, (("patch", 0),), patch_rows)
    before = framed[:patch_rows]
    after = framed[2 * patch_rows :]
    fresh = interleaved([query, fresh_key, fresh_value])
    first_tile = (lax.axis_index("patch") - 1) * per_patch
    local_ids = (key_tiles - first_tile).astype(jnp.int32)
    merged = tile_attention(
        fresh, before, after, local_ids, tile_count.astype(jnp.int32), local_heads, per_patch
    )
    return lax.all_to_all(merged, "seq", split_axis=0, concat_axis=1, tiled=True)


def solution(mesh):
    return jax.shard_map(
        on_device,
        mesh=mesh,
        in_specs=(
            P(("cfg", "patch", "seq"), None),
            P(("cfg", "patch", "seq"), None),
            P(("cfg", "patch", "seq"), None),
            P(("cfg", "patch", "seq"), None),
            P(("cfg", "patch", "seq"), None),
            P("patch", None),
            P("patch"),
        ),
        out_specs=P(("cfg", "patch", "seq"), None),
        check_vma=False,
    )
```

```python
import functools

import jax
import jax.numpy as jnp
from jax import lax
from jax.experimental import pallas as pl
from jax.experimental.pallas import tpu as pltpu
from jax.sharding import PartitionSpec as P

NUM_HEADS = 16
HEAD_DIM = 128
TILE_TOKENS = 384
TILES_H = 2
TILES_W = 3
KEY_SLOTS = 18
SLOT_GROUP = 3


soft_cap = 8.0


def with_halo(x, sides, width):
    for axis, dim in sides:
        size, length = (lax.axis_size(axis), x.shape[dim])
        up = [(i, (i + 1) % size) for i in range(size - 1)]
        down = [(j, i) for i, j in up]
        last = lax.slice_in_dim(x, length - width, length, axis=dim)
        leading = lax.slice_in_dim(x, 0, width, axis=dim)
        before = lax.ppermute(last, axis, up)
        after = lax.ppermute(leading, axis, down)
        x = jnp.concatenate([before, x, after], axis=dim)
    return x


def attention_kernel(local_heads, per_patch, stale_phase, ids_ref, count_ref, fresh_ref, *refs):
    if stale_phase:
        before_hbm, after_hbm, acc_in, tot_in, o_ref, stale_ref, copy_sem, list_ref, acc_ref, tot_ref = refs
        keys_ref = stale_ref
    else:
        acc_ref, tot_ref, list_ref = refs
        keys_ref = fresh_ref
    t = pl.program_id(0)
    width = local_heads * HEAD_DIM
    patch_rows = fresh_ref.shape[0]
    factor = 1.0 / (HEAD_DIM**0.5) / soft_cap
    lift = soft_cap * 1.4426950408889634

    if stale_phase:

        @pl.when(t == 0)
        def _():
            first = pltpu.make_async_copy(before_hbm, stale_ref.at[pl.ds(0, patch_rows)], copy_sem.at[0])
            second = pltpu.make_async_copy(
                after_hbm, stale_ref.at[pl.ds(patch_rows, patch_rows)], copy_sem.at[1]
            )
            first.start()
            second.start()
            first.wait()
            second.wait()

    def compact(j, n):
        u = ids_ref[t, j]
        which = u // per_patch
        row = u - which * per_patch
        if stale_phase:
            keep = which != 1
            index = (which // 2) * per_patch + row
        else:
            keep = which == 1
            index = row

        @pl.when(keep)
        def _():
            list_ref[n] = index

        return n + keep.astype(jnp.int32)

    used = lax.fori_loop(0, count_ref[t], compact, jnp.int32(0))

    for h in range(local_heads):
        head = pl.ds(h * HEAD_DIM, HEAD_DIM)
        start_q = pl.multiple_of(t * TILE_TOKENS, TILE_TOKENS)
        query = fresh_ref[pl.ds(start_q, TILE_TOKENS), pl.ds(h * HEAD_DIM, HEAD_DIM)]
        if stale_phase:
            acc_ref[...] = acc_in[:, head]
            tot_ref[...] = tot_in[:, head]
            k_col, v_col = h * HEAD_DIM, width + h * HEAD_DIM
        else:
            acc_ref[:, head] = jnp.zeros((TILE_TOKENS, HEAD_DIM), jnp.float32)
            tot_ref[:, head] = jnp.zeros((TILE_TOKENS, HEAD_DIM), jnp.float32)
            k_col, v_col = width + h * HEAD_DIM, 2 * width + h * HEAD_DIM
        acc_at = slice(None) if stale_phase else head

        def weights(index):
            start = pl.multiple_of(index * TILE_TOKENS, TILE_TOKENS)
            keys = keys_ref[pl.ds(start, TILE_TOKENS), pl.ds(k_col, HEAD_DIM)]
            values = keys_ref[pl.ds(start, TILE_TOKENS), pl.ds(v_col, HEAD_DIM)]
            scores = lax.dot_general(
                query, keys, (((1,), (1,)), ((), ())), preferred_element_type=jnp.float32
            )
            weight = jnp.exp2(jnp.tanh(scores * factor) * lift - lift)
            part = weight[:, 0:HEAD_DIM]
            for c in range(1, TILE_TOKENS // HEAD_DIM):
                part = part + weight[:, c * HEAD_DIM:(c + 1) * HEAD_DIM]
            return weight.astype(jnp.bfloat16), part, values

        def accumulate(indices):
            got = [weights(i) for i in indices]
            part = got[0][1]
            for g in got[1:]:
                part = part + g[1]
            tot_ref[:, acc_at] += part
            acc_ref[:, acc_at] += jnp.dot(
                jnp.concatenate([g[0] for g in got], axis=1),
                jnp.concatenate([g[2] for g in got], axis=0),
                preferred_element_type=jnp.float32,
            )

        def group(p, carry):
            accumulate([list_ref[SLOT_GROUP * p + i] for i in range(SLOT_GROUP)])
            return carry

        lax.fori_loop(0, used // SLOT_GROUP, group, 0)
        for left in range(1, SLOT_GROUP):

            @pl.when(used % SLOT_GROUP == left)
            def _():
                accumulate([list_ref[used - left + i] for i in range(left)])

        if stale_phase:
            total = jnp.sum(tot_ref[...], axis=1, keepdims=True)
            o_ref[:, head] = (acc_ref[...] / total).astype(o_ref.dtype)


def tile_attention(fresh, before, after, local_ids, tile_count, local_heads, per_patch):
    rows = fresh.shape[0]
    width = local_heads * HEAD_DIM
    tiles = rows // TILE_TOKENS

    def whole(array):
        return pl.BlockSpec(array.shape, lambda t, ids, cnt: (0, 0))

    fresh = pltpu.with_memory_space_constraint(fresh, pltpu.VMEM)
    resident = pl.BlockSpec(memory_space=pltpu.VMEM)

    tile = pl.BlockSpec((TILE_TOKENS, width), lambda t, ids, cnt: (t, 0))
    partial = jax.ShapeDtypeStruct((rows, width), jnp.float32)
    acc, tot = pl.pallas_call(
        functools.partial(attention_kernel, local_heads, per_patch, False),
        out_shape=(partial, partial),
        grid_spec=pltpu.PrefetchScalarGridSpec(
            num_scalar_prefetch=2,
            grid=(tiles,),
            in_specs=[resident],
            out_specs=(tile, tile),
            scratch_shapes=[pltpu.SMEM((KEY_SLOTS,), jnp.int32)],
        ),
    )(local_ids, tile_count, fresh)
    hbm = pl.BlockSpec(memory_space=pl.ANY)
    return pl.pallas_call(
        functools.partial(attention_kernel, local_heads, per_patch, True),
        out_shape=jax.ShapeDtypeStruct((rows, width), jnp.bfloat16),
        grid_spec=pltpu.PrefetchScalarGridSpec(
            num_scalar_prefetch=2,
            grid=(tiles,),
            in_specs=[resident, hbm, hbm, tile, tile],
            out_specs=tile,
            scratch_shapes=[
                pltpu.VMEM((2 * rows, before.shape[1]), before.dtype),
                pltpu.SemaphoreType.DMA((2,)),
                pltpu.SMEM((KEY_SLOTS,), jnp.int32),
                pltpu.VMEM((TILE_TOKENS, HEAD_DIM), jnp.float32),
                pltpu.VMEM((TILE_TOKENS, HEAD_DIM), jnp.float32),
            ],
        ),
        compiler_params=pltpu.CompilerParams(dimension_semantics=("arbitrary",)),
    )(local_ids, tile_count, fresh, before, after, acc, tot)


def regroup_kernel(width, *refs):
    *in_refs, o_ref = refs
    seq_count = o_ref.shape[0]
    for d in range(seq_count):
        for a, ref in enumerate(in_refs):
            o_ref[d, :, a * width:(a + 1) * width] = ref[:, d * width:(d + 1) * width]


def regroup(arrays, seq_count, width):
    rows = arrays[0].shape[0]
    return pl.pallas_call(
        functools.partial(regroup_kernel, width),
        out_shape=jax.ShapeDtypeStruct((seq_count, rows, len(arrays) * width), arrays[0].dtype),
    )(*arrays)


def pass_kernel(x_ref, o_ref):
    o_ref[...] = x_ref[...]


def out_of_vmem(x):
    x = pltpu.with_memory_space_constraint(x, pltpu.VMEM)
    return pl.pallas_call(
        pass_kernel,
        out_shape=jax.ShapeDtypeStruct(x.shape, x.dtype),
        in_specs=[pl.BlockSpec(memory_space=pltpu.VMEM)],
    )(x)


def on_device(query, fresh_key, fresh_value, stale_key, stale_value, key_tiles, tile_count):
    seq_count = lax.axis_size("seq")
    local_heads = NUM_HEADS // seq_count
    width = local_heads * HEAD_DIM
    per_patch = TILES_H * TILES_W
    rows = query.shape[0]
    patch_rows = rows * seq_count

    def interleaved(arrays):
        parts = [a.reshape(rows, seq_count, width) for a in arrays]
        joined = jnp.concatenate(parts, axis=2).transpose(1, 0, 2)
        moved = lax.all_to_all(joined, "seq", split_axis=0, concat_axis=0, tiled=True)
        return moved.reshape(patch_rows, len(arrays) * width)

    joined = regroup([stale_key, stale_value], seq_count, width)
    stale = lax.all_to_all(joined, "seq", split_axis=0, concat_axis=0, tiled=True)
    stale = out_of_vmem(stale.reshape(patch_rows, 2 * width))
    framed = with_halo(stale, (("patch", 0),), patch_rows)
    before = framed[:patch_rows]
    after = framed[2 * patch_rows :]
    fresh = interleaved([query, fresh_key, fresh_value])
    first_tile = (lax.axis_index("patch") - 1) * per_patch
    local_ids = (key_tiles - first_tile).astype(jnp.int32)
    merged = tile_attention(
        fresh, before, after, local_ids, tile_count.astype(jnp.int32), local_heads, per_patch
    )
    return lax.all_to_all(merged, "seq", split_axis=0, concat_axis=1, tiled=True)


def solution(mesh):
    return jax.shard_map(
        on_device,
        mesh=mesh,
        in_specs=(
            P(("cfg", "patch", "seq"), None),
            P(("cfg", "patch", "seq"), None),
            P(("cfg", "patch", "seq"), None),
            P(("cfg", "patch", "seq"), None),
            P(("cfg", "patch", "seq"), None),
            P("patch", None),
            P("patch"),
        ),
        out_specs=P(("cfg", "patch", "seq"), None),
        check_vma=False,
    )
```

```python
import functools

import jax
import jax.numpy as jnp
from jax import lax
from jax.experimental import pallas as pl
from jax.experimental.pallas import tpu as pltpu
from jax.sharding import PartitionSpec as P

NUM_HEADS = 16
HEAD_DIM = 128
TILE_TOKENS = 384
TILES_H = 2
TILES_W = 3
KEY_SLOTS = 18
SLOT_GROUP = 3


soft_cap = 8.0


def with_halo(x, sides, width):
    for axis, dim in sides:
        size, length = (lax.axis_size(axis), x.shape[dim])
        up = [(i, (i + 1) % size) for i in range(size - 1)]
        down = [(j, i) for i, j in up]
        last = lax.slice_in_dim(x, length - width, length, axis=dim)
        leading = lax.slice_in_dim(x, 0, width, axis=dim)
        before = lax.ppermute(last, axis, up)
        after = lax.ppermute(leading, axis, down)
        x = jnp.concatenate([before, x, after], axis=dim)
    return x


def attention_kernel(local_heads, per_patch, stale_phase, ids_ref, count_ref, fresh_ref, *refs):
    if stale_phase:
        before_hbm, after_hbm, acc_in, tot_in, o_ref, stale_ref, copy_sem, list_ref, acc_ref, tot_ref = refs
        keys_ref = stale_ref
    else:
        acc_ref, tot_ref, list_ref = refs
        keys_ref = fresh_ref
    t = pl.program_id(0)
    width = local_heads * HEAD_DIM
    patch_rows = fresh_ref.shape[0]
    factor = 1.0 / (HEAD_DIM**0.5) / soft_cap
    lift = soft_cap * 1.4426950408889634

    if stale_phase:

        @pl.when(t == 0)
        def _():
            first = pltpu.make_async_copy(before_hbm, stale_ref.at[pl.ds(0, patch_rows)], copy_sem.at[0])
            second = pltpu.make_async_copy(
                after_hbm, stale_ref.at[pl.ds(patch_rows, patch_rows)], copy_sem.at[1]
            )
            first.start()
            second.start()
            first.wait()
            second.wait()

    def compact(j, n):
        u = ids_ref[t, j]
        which = u // per_patch
        row = u - which * per_patch
        if stale_phase:
            keep = which != 1
            index = (which // 2) * per_patch + row
        else:
            keep = which == 1
            index = row

        @pl.when(keep)
        def _():
            list_ref[n] = index

        return n + keep.astype(jnp.int32)

    used = lax.fori_loop(0, count_ref[t], compact, jnp.int32(0))

    for h in range(local_heads):
        head = pl.ds(h * HEAD_DIM, HEAD_DIM)
        start_q = pl.multiple_of(t * TILE_TOKENS, TILE_TOKENS)
        query = fresh_ref[pl.ds(start_q, TILE_TOKENS), pl.ds(h * HEAD_DIM, HEAD_DIM)]
        if stale_phase:
            acc_ref[...] = acc_in[:, head]
            tot_ref[...] = tot_in[:, head]
            k_col, v_col = h * HEAD_DIM, width + h * HEAD_DIM
        else:
            acc_ref[:, head] = jnp.zeros((TILE_TOKENS, HEAD_DIM), jnp.float32)
            tot_ref[:, head] = jnp.zeros((TILE_TOKENS, HEAD_DIM), jnp.float32)
            k_col, v_col = width + h * HEAD_DIM, 2 * width + h * HEAD_DIM
        acc_at = slice(None) if stale_phase else head

        def accumulate(indices):
            starts = [pl.multiple_of(i * TILE_TOKENS, TILE_TOKENS) for i in indices]
            keys = jnp.concatenate(
                [keys_ref[pl.ds(a, TILE_TOKENS), pl.ds(k_col, HEAD_DIM)] for a in starts], axis=0
            )
            values = jnp.concatenate(
                [keys_ref[pl.ds(a, TILE_TOKENS), pl.ds(v_col, HEAD_DIM)] for a in starts], axis=0
            )
            scores = lax.dot_general(
                query, keys, (((1,), (1,)), ((), ())), preferred_element_type=jnp.float32
            )
            weight = jnp.exp2(jnp.tanh(scores * factor) * lift - lift)
            part = weight[:, 0:HEAD_DIM]
            for c in range(1, weight.shape[1] // HEAD_DIM):
                part = part + weight[:, c * HEAD_DIM:(c + 1) * HEAD_DIM]
            tot_ref[:, acc_at] += part
            acc_ref[:, acc_at] += jnp.dot(
                weight.astype(jnp.bfloat16), values, preferred_element_type=jnp.float32
            )

        def group(p, carry):
            accumulate([list_ref[SLOT_GROUP * p + i] for i in range(SLOT_GROUP)])
            return carry

        lax.fori_loop(0, used // SLOT_GROUP, group, 0)
        for left in range(1, SLOT_GROUP):

            @pl.when(used % SLOT_GROUP == left)
            def _():
                accumulate([list_ref[used - left + i] for i in range(left)])

        if stale_phase:
            total = jnp.sum(tot_ref[...], axis=1, keepdims=True)
            o_ref[:, head] = (acc_ref[...] / total).astype(o_ref.dtype)


def tile_attention(fresh, before, after, local_ids, tile_count, local_heads, per_patch):
    rows = fresh.shape[0]
    width = local_heads * HEAD_DIM
    tiles = rows // TILE_TOKENS

    def whole(array):
        return pl.BlockSpec(array.shape, lambda t, ids, cnt: (0, 0))

    fresh = pltpu.with_memory_space_constraint(fresh, pltpu.VMEM)
    resident = pl.BlockSpec(memory_space=pltpu.VMEM)

    tile = pl.BlockSpec((TILE_TOKENS, width), lambda t, ids, cnt: (t, 0))
    partial = jax.ShapeDtypeStruct((rows, width), jnp.float32)
    acc, tot = pl.pallas_call(
        functools.partial(attention_kernel, local_heads, per_patch, False),
        out_shape=(partial, partial),
        grid_spec=pltpu.PrefetchScalarGridSpec(
            num_scalar_prefetch=2,
            grid=(tiles,),
            in_specs=[resident],
            out_specs=(tile, tile),
            scratch_shapes=[pltpu.SMEM((KEY_SLOTS,), jnp.int32)],
        ),
    )(local_ids, tile_count, fresh)
    hbm = pl.BlockSpec(memory_space=pl.ANY)
    return pl.pallas_call(
        functools.partial(attention_kernel, local_heads, per_patch, True),
        out_shape=jax.ShapeDtypeStruct((rows, width), jnp.bfloat16),
        grid_spec=pltpu.PrefetchScalarGridSpec(
            num_scalar_prefetch=2,
            grid=(tiles,),
            in_specs=[resident, hbm, hbm, tile, tile],
            out_specs=tile,
            scratch_shapes=[
                pltpu.VMEM((2 * rows, before.shape[1]), before.dtype),
                pltpu.SemaphoreType.DMA((2,)),
                pltpu.SMEM((KEY_SLOTS,), jnp.int32),
                pltpu.VMEM((TILE_TOKENS, HEAD_DIM), jnp.float32),
                pltpu.VMEM((TILE_TOKENS, HEAD_DIM), jnp.float32),
            ],
        ),
        compiler_params=pltpu.CompilerParams(dimension_semantics=("arbitrary",)),
    )(local_ids, tile_count, fresh, before, after, acc, tot)


def regroup_kernel(width, *refs):
    *in_refs, o_ref = refs
    seq_count = o_ref.shape[0]
    for d in range(seq_count):
        for a, ref in enumerate(in_refs):
            o_ref[d, :, a * width:(a + 1) * width] = ref[:, d * width:(d + 1) * width]


def regroup(arrays, seq_count, width):
    rows = arrays[0].shape[0]
    return pl.pallas_call(
        functools.partial(regroup_kernel, width),
        out_shape=jax.ShapeDtypeStruct((seq_count, rows, len(arrays) * width), arrays[0].dtype),
    )(*arrays)


def on_device(query, fresh_key, fresh_value, stale_key, stale_value, key_tiles, tile_count):
    seq_count = lax.axis_size("seq")
    local_heads = NUM_HEADS // seq_count
    width = local_heads * HEAD_DIM
    per_patch = TILES_H * TILES_W
    rows = query.shape[0]
    patch_rows = rows * seq_count

    def interleaved(arrays):
        parts = [a.reshape(rows, seq_count, width) for a in arrays]
        joined = jnp.concatenate(parts, axis=2).transpose(1, 0, 2)
        moved = lax.all_to_all(joined, "seq", split_axis=0, concat_axis=0, tiled=True)
        return moved.reshape(patch_rows, len(arrays) * width)

    joined = regroup([stale_key, stale_value], seq_count, width)
    stale = lax.all_to_all(joined, "seq", split_axis=0, concat_axis=0, tiled=True)
    stale = stale.reshape(patch_rows, 2 * width)
    framed = with_halo(stale, (("patch", 0),), patch_rows)
    before = framed[:patch_rows]
    after = framed[2 * patch_rows :]
    fresh = interleaved([query, fresh_key, fresh_value])
    first_tile = (lax.axis_index("patch") - 1) * per_patch
    local_ids = (key_tiles - first_tile).astype(jnp.int32)
    merged = tile_attention(
        fresh, before, after, local_ids, tile_count.astype(jnp.int32), local_heads, per_patch
    )
    return lax.all_to_all(merged, "seq", split_axis=0, concat_axis=1, tiled=True)


def solution(mesh):
    return jax.shard_map(
        on_device,
        mesh=mesh,
        in_specs=(
            P(("cfg", "patch", "seq"), None),
            P(("cfg", "patch", "seq"), None),
            P(("cfg", "patch", "seq"), None),
            P(("cfg", "patch", "seq"), None),
            P(("cfg", "patch", "seq"), None),
            P("patch", None),
            P("patch"),
        ),
        out_specs=P(("cfg", "patch", "seq"), None),
        check_vma=False,
    )
```

```python
import functools

import jax
import jax.numpy as jnp
from jax import lax
from jax.experimental import pallas as pl
from jax.experimental.pallas import tpu as pltpu
from jax.sharding import PartitionSpec as P

NUM_HEADS = 16
HEAD_DIM = 128
TILE_TOKENS = 384
TILES_H = 2
TILES_W = 3
KEY_SLOTS = 18
SLOT_GROUP = 3


soft_cap = 8.0


def with_halo(x, sides, width):
    for axis, dim in sides:
        size, length = (lax.axis_size(axis), x.shape[dim])
        up = [(i, (i + 1) % size) for i in range(size - 1)]
        down = [(j, i) for i, j in up]
        last = lax.slice_in_dim(x, length - width, length, axis=dim)
        leading = lax.slice_in_dim(x, 0, width, axis=dim)
        before = lax.ppermute(last, axis, up)
        after = lax.ppermute(leading, axis, down)
        x = jnp.concatenate([before, x, after], axis=dim)
    return x


def attention_kernel(local_heads, per_patch, stale_phase, ids_ref, count_ref, fresh_ref, *refs):
    if stale_phase:
        before_hbm, after_hbm, acc_in, tot_in, o_ref, stale_ref, copy_sem, list_ref, acc_ref, tot_ref = refs
        keys_ref = stale_ref
    else:
        acc_ref, tot_ref, list_ref = refs
        keys_ref = fresh_ref
    t = pl.program_id(0)
    width = local_heads * HEAD_DIM
    patch_rows = fresh_ref.shape[0]
    factor = 1.0 / (HEAD_DIM**0.5) / soft_cap
    lift = soft_cap * 1.4426950408889634

    if stale_phase:

        @pl.when(t == 0)
        def _():
            first = pltpu.make_async_copy(before_hbm, stale_ref.at[pl.ds(0, patch_rows)], copy_sem.at[0])
            second = pltpu.make_async_copy(
                after_hbm, stale_ref.at[pl.ds(patch_rows, patch_rows)], copy_sem.at[1]
            )
            first.start()
            second.start()
            first.wait()
            second.wait()

    def compact(j, n):
        u = ids_ref[t, j]
        which = u // per_patch
        row = u - which * per_patch
        if stale_phase:
            keep = which != 1
            index = (which // 2) * per_patch + row
        else:
            keep = which == 1
            index = row

        @pl.when(keep)
        def _():
            list_ref[n] = index

        return n + keep.astype(jnp.int32)

    used = lax.fori_loop(0, count_ref[t], compact, jnp.int32(0))

    for h in range(local_heads):
        head = pl.ds(h * HEAD_DIM, HEAD_DIM)
        start_q = pl.multiple_of(t * TILE_TOKENS, TILE_TOKENS)
        query = fresh_ref[pl.ds(start_q, TILE_TOKENS), pl.ds(h * HEAD_DIM, HEAD_DIM)]
        if stale_phase:
            acc_ref[...] = acc_in[:, head]
            tot_ref[...] = tot_in[:, head]
            k_col, v_col = h * HEAD_DIM, width + h * HEAD_DIM
        else:
            acc_ref[:, head] = jnp.zeros((TILE_TOKENS, HEAD_DIM), jnp.float32)
            tot_ref[:, head] = jnp.zeros((TILE_TOKENS, HEAD_DIM), jnp.float32)
            k_col, v_col = width + h * HEAD_DIM, 2 * width + h * HEAD_DIM
        acc_at = slice(None) if stale_phase else head

        def weights(index):
            start = pl.multiple_of(index * TILE_TOKENS, TILE_TOKENS)
            keys = keys_ref[pl.ds(start, TILE_TOKENS), pl.ds(k_col, HEAD_DIM)]
            values = keys_ref[pl.ds(start, TILE_TOKENS), pl.ds(v_col, HEAD_DIM)]
            scores = lax.dot_general(
                query, keys, (((1,), (1,)), ((), ())), preferred_element_type=jnp.float32
            )
            weight = jnp.exp2(jnp.tanh(scores * factor) * lift - lift)
            part = weight[:, 0:HEAD_DIM]
            for c in range(1, TILE_TOKENS // HEAD_DIM):
                part = part + weight[:, c * HEAD_DIM:(c + 1) * HEAD_DIM]
            return weight.astype(jnp.bfloat16), part, values

        def accumulate(indices):
            got = [weights(i) for i in indices]
            part = got[0][1]
            for g in got[1:]:
                part = part + g[1]
            tot_ref[:, acc_at] += part
            acc_ref[:, acc_at] += jnp.dot(
                jnp.concatenate([g[0] for g in got], axis=1),
                jnp.concatenate([g[2] for g in got], axis=0),
                preferred_element_type=jnp.float32,
            )

        def group(p, carry):
            accumulate([list_ref[SLOT_GROUP * p + i] for i in range(SLOT_GROUP)])
            return carry

        lax.fori_loop(0, used // SLOT_GROUP, group, 0)
        for left in range(1, SLOT_GROUP):

            @pl.when(used % SLOT_GROUP == left)
            def _():
                accumulate([list_ref[used - left + i] for i in range(left)])

        if stale_phase:
            total = jnp.sum(tot_ref[...], axis=1, keepdims=True)
            o_ref[:, head] = (acc_ref[...] / total).astype(o_ref.dtype)


def tile_attention(fresh, before, after, local_ids, tile_count, local_heads, per_patch):
    rows = fresh.shape[0]
    width = local_heads * HEAD_DIM
    tiles = rows // TILE_TOKENS

    def whole(array):
        return pl.BlockSpec(array.shape, lambda t, ids, cnt: (0, 0))

    fresh = pltpu.with_memory_space_constraint(fresh, pltpu.VMEM)
    after = pltpu.with_memory_space_constraint(after, pltpu.VMEM)
    resident = pl.BlockSpec(memory_space=pltpu.VMEM)

    tile = pl.BlockSpec((TILE_TOKENS, width), lambda t, ids, cnt: (t, 0))
    partial = jax.ShapeDtypeStruct((rows, width), jnp.float32)
    acc, tot = pl.pallas_call(
        functools.partial(attention_kernel, local_heads, per_patch, False),
        out_shape=(partial, partial),
        grid_spec=pltpu.PrefetchScalarGridSpec(
            num_scalar_prefetch=2,
            grid=(tiles,),
            in_specs=[resident],
            out_specs=(tile, tile),
            scratch_shapes=[pltpu.SMEM((KEY_SLOTS,), jnp.int32)],
        ),
    )(local_ids, tile_count, fresh)
    hbm = pl.BlockSpec(memory_space=pl.ANY)
    return pl.pallas_call(
        functools.partial(attention_kernel, local_heads, per_patch, True),
        out_shape=jax.ShapeDtypeStruct((rows, width), jnp.bfloat16),
        grid_spec=pltpu.PrefetchScalarGridSpec(
            num_scalar_prefetch=2,
            grid=(tiles,),
            in_specs=[resident, hbm, resident, tile, tile],
            out_specs=tile,
            scratch_shapes=[
                pltpu.VMEM((2 * rows, before.shape[1]), before.dtype),
                pltpu.SemaphoreType.DMA((2,)),
                pltpu.SMEM((KEY_SLOTS,), jnp.int32),
                pltpu.VMEM((TILE_TOKENS, HEAD_DIM), jnp.float32),
                pltpu.VMEM((TILE_TOKENS, HEAD_DIM), jnp.float32),
            ],
        ),
        compiler_params=pltpu.CompilerParams(dimension_semantics=("arbitrary",)),
    )(local_ids, tile_count, fresh, before, after, acc, tot)


def regroup_kernel(width, *refs):
    *in_refs, o_ref = refs
    seq_count = o_ref.shape[0]
    for d in range(seq_count):
        for a, ref in enumerate(in_refs):
            o_ref[d, :, a * width:(a + 1) * width] = ref[:, d * width:(d + 1) * width]


def regroup(arrays, seq_count, width):
    rows = arrays[0].shape[0]
    return pl.pallas_call(
        functools.partial(regroup_kernel, width),
        out_shape=jax.ShapeDtypeStruct((seq_count, rows, len(arrays) * width), arrays[0].dtype),
    )(*arrays)


def on_device(query, fresh_key, fresh_value, stale_key, stale_value, key_tiles, tile_count):
    seq_count = lax.axis_size("seq")
    local_heads = NUM_HEADS // seq_count
    width = local_heads * HEAD_DIM
    per_patch = TILES_H * TILES_W
    rows = query.shape[0]
    patch_rows = rows * seq_count

    def interleaved(arrays):
        parts = [a.reshape(rows, seq_count, width) for a in arrays]
        joined = jnp.concatenate(parts, axis=2).transpose(1, 0, 2)
        moved = lax.all_to_all(joined, "seq", split_axis=0, concat_axis=0, tiled=True)
        return moved.reshape(patch_rows, len(arrays) * width)

    joined = regroup([stale_key, stale_value], seq_count, width)
    stale = lax.all_to_all(joined, "seq", split_axis=0, concat_axis=0, tiled=True)
    stale = stale.reshape(patch_rows, 2 * width)
    framed = with_halo(stale, (("patch", 0),), patch_rows)
    before = framed[:patch_rows]
    after = framed[2 * patch_rows :]
    fresh = interleaved([query, fresh_key, fresh_value])
    first_tile = (lax.axis_index("patch") - 1) * per_patch
    local_ids = (key_tiles - first_tile).astype(jnp.int32)
    merged = tile_attention(
        fresh, before, after, local_ids, tile_count.astype(jnp.int32), local_heads, per_patch
    )
    return lax.all_to_all(merged, "seq", split_axis=0, concat_axis=1, tiled=True)


def solution(mesh):
    return jax.shard_map(
        on_device,
        mesh=mesh,
        in_specs=(
            P(("cfg", "patch", "seq"), None),
            P(("cfg", "patch", "seq"), None),
            P(("cfg", "patch", "seq"), None),
            P(("cfg", "patch", "seq"), None),
            P(("cfg", "patch", "seq"), None),
            P("patch", None),
            P("patch"),
        ),
        out_specs=P(("cfg", "patch", "seq"), None),
        check_vma=False,
    )
```

```python
import functools

import jax
import jax.numpy as jnp
from jax import lax
from jax.experimental import pallas as pl
from jax.experimental.pallas import tpu as pltpu
from jax.sharding import PartitionSpec as P

NUM_HEADS = 16
HEAD_DIM = 128
TILE_TOKENS = 384
TILES_H = 2
TILES_W = 3
KEY_SLOTS = 18
SLOT_GROUP = 3


soft_cap = 8.0


def with_halo(x, sides, width):
    for axis, dim in sides:
        size, length = (lax.axis_size(axis), x.shape[dim])
        up = [(i, (i + 1) % size) for i in range(size - 1)]
        down = [(j, i) for i, j in up]
        last = lax.slice_in_dim(x, length - width, length, axis=dim)
        leading = lax.slice_in_dim(x, 0, width, axis=dim)
        before = lax.ppermute(last, axis, up)
        after = lax.ppermute(leading, axis, down)
        x = jnp.concatenate([before, x, after], axis=dim)
    return x


def attention_kernel(local_heads, per_patch, stale_phase, ids_ref, count_ref, fresh_ref, *refs):
    if stale_phase:
        before_hbm, after_hbm, acc_in, tot_in, o_ref, stale_ref, copy_sem, list_ref, acc_ref, tot_ref = refs
        keys_ref = stale_ref
    else:
        acc_ref, tot_ref, list_ref = refs
        keys_ref = fresh_ref
    t = pl.program_id(0)
    width = local_heads * HEAD_DIM
    patch_rows = fresh_ref.shape[0]
    factor = 1.0 / (HEAD_DIM**0.5) / soft_cap
    lift = soft_cap * 1.4426950408889634

    if stale_phase:

        @pl.when(t == 0)
        def _():
            first = pltpu.make_async_copy(before_hbm, stale_ref.at[pl.ds(0, patch_rows)], copy_sem.at[0])
            second = pltpu.make_async_copy(
                after_hbm, stale_ref.at[pl.ds(patch_rows, patch_rows)], copy_sem.at[1]
            )
            first.start()
            second.start()
            first.wait()
            second.wait()

    def compact(j, n):
        u = ids_ref[t, j]
        which = u // per_patch
        row = u - which * per_patch
        if stale_phase:
            keep = which != 1
            index = (which // 2) * per_patch + row
        else:
            keep = which == 1
            index = row

        @pl.when(keep)
        def _():
            list_ref[n] = index

        return n + keep.astype(jnp.int32)

    used = lax.fori_loop(0, count_ref[t], compact, jnp.int32(0))

    for h in range(local_heads):
        head = pl.ds(h * HEAD_DIM, HEAD_DIM)
        start_q = pl.multiple_of(t * TILE_TOKENS, TILE_TOKENS)
        query = fresh_ref[pl.ds(start_q, TILE_TOKENS), pl.ds(h * HEAD_DIM, HEAD_DIM)]
        if stale_phase:
            acc_ref[...] = acc_in[:, head]
            tot_ref[...] = tot_in[:, head]
            k_col, v_col = h * HEAD_DIM, width + h * HEAD_DIM
        else:
            acc_ref[:, head] = jnp.zeros((TILE_TOKENS, HEAD_DIM), jnp.float32)
            tot_ref[:, head] = jnp.zeros((TILE_TOKENS, HEAD_DIM), jnp.float32)
            k_col, v_col = width + h * HEAD_DIM, 2 * width + h * HEAD_DIM
        acc_at = slice(None) if stale_phase else head

        def weights(index):
            start = pl.multiple_of(index * TILE_TOKENS, TILE_TOKENS)
            keys = keys_ref[pl.ds(start, TILE_TOKENS), pl.ds(k_col, HEAD_DIM)]
            values = keys_ref[pl.ds(start, TILE_TOKENS), pl.ds(v_col, HEAD_DIM)]
            scores = lax.dot_general(
                query, keys, (((1,), (1,)), ((), ())), preferred_element_type=jnp.float32
            )
            weight = jnp.exp2(jnp.tanh(scores * factor) * lift - lift)
            part = weight[:, 0:HEAD_DIM]
            for c in range(1, TILE_TOKENS // HEAD_DIM):
                part = part + weight[:, c * HEAD_DIM:(c + 1) * HEAD_DIM]
            return weight.astype(jnp.bfloat16), part, values

        def accumulate(indices):
            got = [weights(i) for i in indices]
            part = got[0][1]
            for g in got[1:]:
                part = part + g[1]
            tot_ref[:, acc_at] += part
            acc_ref[:, acc_at] += jnp.dot(
                jnp.concatenate([g[0] for g in got], axis=1),
                jnp.concatenate([g[2] for g in got], axis=0),
                preferred_element_type=jnp.float32,
            )

        def group(p, carry):
            accumulate([list_ref[SLOT_GROUP * p + i] for i in range(SLOT_GROUP)])
            return carry

        lax.fori_loop(0, used // SLOT_GROUP, group, 0)
        for left in range(1, SLOT_GROUP):

            @pl.when(used % SLOT_GROUP == left)
            def _():
                accumulate([list_ref[used - left + i] for i in range(left)])

        if stale_phase:
            total = jnp.sum(tot_ref[...], axis=1, keepdims=True)
            o_ref[:, head] = (acc_ref[...] / total).astype(o_ref.dtype)


def tile_attention(fresh, before, after, local_ids, tile_count, local_heads, per_patch):
    rows = fresh.shape[0]
    width = local_heads * HEAD_DIM
    tiles = rows // TILE_TOKENS

    def whole(array):
        return pl.BlockSpec(array.shape, lambda t, ids, cnt: (0, 0))

    fresh = pltpu.with_memory_space_constraint(fresh, pltpu.VMEM)
    after = pltpu.with_memory_space_constraint(after, pltpu.VMEM)
    resident = pl.BlockSpec(memory_space=pltpu.VMEM)

    tile = pl.BlockSpec((TILE_TOKENS, width), lambda t, ids, cnt: (t, 0))
    partial = jax.ShapeDtypeStruct((rows, width), jnp.float32)
    acc, tot = pl.pallas_call(
        functools.partial(attention_kernel, local_heads, per_patch, False),
        out_shape=(partial, partial),
        grid_spec=pltpu.PrefetchScalarGridSpec(
            num_scalar_prefetch=2,
            grid=(tiles,),
            in_specs=[resident],
            out_specs=(tile, tile),
            scratch_shapes=[pltpu.SMEM((KEY_SLOTS,), jnp.int32)],
        ),
    )(local_ids, tile_count, fresh)
    hbm = pl.BlockSpec(memory_space=pl.ANY)
    return pl.pallas_call(
        functools.partial(attention_kernel, local_heads, per_patch, True),
        out_shape=jax.ShapeDtypeStruct((rows, width), jnp.bfloat16),
        grid_spec=pltpu.PrefetchScalarGridSpec(
            num_scalar_prefetch=2,
            grid=(tiles,),
            in_specs=[resident, hbm, resident, tile, tile],
            out_specs=tile,
            scratch_shapes=[
                pltpu.VMEM((2 * rows, before.shape[1]), before.dtype),
                pltpu.SemaphoreType.DMA((2,)),
                pltpu.SMEM((KEY_SLOTS,), jnp.int32),
                pltpu.VMEM((TILE_TOKENS, HEAD_DIM), jnp.float32),
                pltpu.VMEM((TILE_TOKENS, HEAD_DIM), jnp.float32),
            ],
        ),
        compiler_params=pltpu.CompilerParams(dimension_semantics=("arbitrary",)),
    )(local_ids, tile_count, fresh, before, after, acc, tot)


def regroup_kernel(width, *refs):
    *in_refs, o_ref, sems = refs
    copies = []
    for d in range(o_ref.shape[0]):
        for a, ref in enumerate(in_refs):
            copy = pltpu.make_async_copy(
                ref.at[:, pl.ds(d * width, width)],
                o_ref.at[d, :, pl.ds(a * width, width)],
                sems.at[d * len(in_refs) + a],
            )
            copy.start()
            copies.append(copy)
    for copy in copies:
        copy.wait()


def regroup(arrays, seq_count, width):
    rows = arrays[0].shape[0]
    anywhere = pl.BlockSpec(memory_space=pl.ANY)
    return pl.pallas_call(
        functools.partial(regroup_kernel, width),
        out_shape=jax.ShapeDtypeStruct((seq_count, rows, len(arrays) * width), arrays[0].dtype),
        in_specs=[anywhere] * len(arrays),
        out_specs=anywhere,
        scratch_shapes=[pltpu.SemaphoreType.DMA((seq_count * len(arrays),))],
    )(*arrays)


def on_device(query, fresh_key, fresh_value, stale_key, stale_value, key_tiles, tile_count):
    seq_count = lax.axis_size("seq")
    local_heads = NUM_HEADS // seq_count
    width = local_heads * HEAD_DIM
    per_patch = TILES_H * TILES_W
    rows = query.shape[0]
    patch_rows = rows * seq_count

    def interleaved(arrays):
        parts = [a.reshape(rows, seq_count, width) for a in arrays]
        joined = jnp.concatenate(parts, axis=2).transpose(1, 0, 2)
        moved = lax.all_to_all(joined, "seq", split_axis=0, concat_axis=0, tiled=True)
        return moved.reshape(patch_rows, len(arrays) * width)

    joined = regroup([stale_key, stale_value], seq_count, width)
    stale = lax.all_to_all(joined, "seq", split_axis=0, concat_axis=0, tiled=True)
    stale = stale.reshape(patch_rows, 2 * width)
    framed = with_halo(stale, (("patch", 0),), patch_rows)
    before = framed[:patch_rows]
    after = framed[2 * patch_rows :]
    fresh = interleaved([query, fresh_key, fresh_value])
    first_tile = (lax.axis_index("patch") - 1) * per_patch
    local_ids = (key_tiles - first_tile).astype(jnp.int32)
    merged = tile_attention(
        fresh, before, after, local_ids, tile_count.astype(jnp.int32), local_heads, per_patch
    )
    return lax.all_to_all(merged, "seq", split_axis=0, concat_axis=1, tiled=True)


def solution(mesh):
    return jax.shard_map(
        on_device,
        mesh=mesh,
        in_specs=(
            P(("cfg", "patch", "seq"), None),
            P(("cfg", "patch", "seq"), None),
            P(("cfg", "patch", "seq"), None),
            P(("cfg", "patch", "seq"), None),
            P(("cfg", "patch", "seq"), None),
            P("patch", None),
            P("patch"),
        ),
        out_specs=P(("cfg", "patch", "seq"), None),
        check_vma=False,
    )
```

```python
import functools

import jax
import jax.numpy as jnp
from jax import lax
from jax.experimental import pallas as pl
from jax.experimental.pallas import tpu as pltpu
from jax.sharding import PartitionSpec as P

NUM_HEADS = 16
HEAD_DIM = 128
TILE_TOKENS = 384
TILES_H = 2
TILES_W = 3
KEY_SLOTS = 18
SLOT_GROUP = 3


soft_cap = 8.0


def with_halo(x, sides, width):
    for axis, dim in sides:
        size, length = (lax.axis_size(axis), x.shape[dim])
        up = [(i, (i + 1) % size) for i in range(size - 1)]
        down = [(j, i) for i, j in up]
        last = lax.slice_in_dim(x, length - width, length, axis=dim)
        leading = lax.slice_in_dim(x, 0, width, axis=dim)
        before = lax.ppermute(last, axis, up)
        after = lax.ppermute(leading, axis, down)
        x = jnp.concatenate([before, x, after], axis=dim)
    return x


def attention_kernel(local_heads, per_patch, stale_phase, ids_ref, count_ref, fresh_ref, *refs):
    if stale_phase:
        before_hbm, after_hbm, acc_in, tot_in, o_ref, stale_ref, copy_sem, list_ref, acc_ref, tot_ref = refs
        keys_ref = stale_ref
    else:
        acc_ref, tot_ref, list_ref = refs
        keys_ref = fresh_ref
    t = pl.program_id(0)
    width = local_heads * HEAD_DIM
    patch_rows = fresh_ref.shape[0]
    factor = 1.0 / (HEAD_DIM**0.5) / soft_cap
    lift = soft_cap * 1.4426950408889634

    if stale_phase:

        @pl.when(t == 0)
        def _():
            first = pltpu.make_async_copy(before_hbm, stale_ref.at[pl.ds(0, patch_rows)], copy_sem.at[0])
            second = pltpu.make_async_copy(
                after_hbm, stale_ref.at[pl.ds(patch_rows, patch_rows)], copy_sem.at[1]
            )
            first.start()
            second.start()
            first.wait()
            second.wait()

    def compact(j, n):
        u = ids_ref[t, j]
        which = u // per_patch
        row = u - which * per_patch
        if stale_phase:
            keep = which != 1
            index = (which // 2) * per_patch + row
        else:
            keep = which == 1
            index = row

        @pl.when(keep)
        def _():
            list_ref[n] = index

        return n + keep.astype(jnp.int32)

    used = lax.fori_loop(0, count_ref[t], compact, jnp.int32(0))

    for h in range(local_heads):
        head = pl.ds(h * HEAD_DIM, HEAD_DIM)
        start_q = pl.multiple_of(t * TILE_TOKENS, TILE_TOKENS)
        query = fresh_ref[pl.ds(start_q, TILE_TOKENS), pl.ds(h * HEAD_DIM, HEAD_DIM)]
        if stale_phase:
            acc_ref[...] = acc_in[:, head]
            tot_ref[...] = tot_in[:, head]
            k_col, v_col = h * HEAD_DIM, width + h * HEAD_DIM
        else:
            acc_ref[:, head] = jnp.zeros((TILE_TOKENS, HEAD_DIM), jnp.float32)
            tot_ref[:, head] = jnp.zeros((TILE_TOKENS, HEAD_DIM), jnp.float32)
            k_col, v_col = width + h * HEAD_DIM, 2 * width + h * HEAD_DIM
        acc_at = slice(None) if stale_phase else head

        def accumulate(indices):
            starts = [pl.multiple_of(i * TILE_TOKENS, TILE_TOKENS) for i in indices]
            keys = jnp.concatenate(
                [keys_ref[pl.ds(a, TILE_TOKENS), pl.ds(k_col, HEAD_DIM)] for a in starts], axis=0
            )
            values = jnp.concatenate(
                [keys_ref[pl.ds(a, TILE_TOKENS), pl.ds(v_col, HEAD_DIM)] for a in starts], axis=0
            )
            scores = lax.dot_general(
                query, keys, (((1,), (1,)), ((), ())), preferred_element_type=jnp.float32
            )
            weight = jnp.exp2(jnp.tanh(scores * factor) * lift - lift)
            part = weight[:, 0:HEAD_DIM]
            for c in range(1, weight.shape[1] // HEAD_DIM):
                part = part + weight[:, c * HEAD_DIM:(c + 1) * HEAD_DIM]
            tot_ref[:, acc_at] += part
            acc_ref[:, acc_at] += jnp.dot(
                weight.astype(jnp.bfloat16), values, preferred_element_type=jnp.float32
            )

        def group(p, carry):
            accumulate([list_ref[SLOT_GROUP * p + i] for i in range(SLOT_GROUP)])
            return carry

        lax.fori_loop(0, used // SLOT_GROUP, group, 0)
        for left in range(1, SLOT_GROUP):

            @pl.when(used % SLOT_GROUP == left)
            def _():
                accumulate([list_ref[used - left + i] for i in range(left)])

        if stale_phase:
            total = jnp.sum(tot_ref[...], axis=1, keepdims=True)
            o_ref[:, head] = (acc_ref[...] / total).astype(o_ref.dtype)


def tile_attention(fresh, before, after, local_ids, tile_count, local_heads, per_patch):
    rows = fresh.shape[0]
    width = local_heads * HEAD_DIM
    tiles = rows // TILE_TOKENS

    def whole(array):
        return pl.BlockSpec(array.shape, lambda t, ids, cnt: (0, 0))

    fresh = pltpu.with_memory_space_constraint(fresh, pltpu.VMEM)
    after = pltpu.with_memory_space_constraint(after, pltpu.VMEM)
    resident = pl.BlockSpec(memory_space=pltpu.VMEM)

    tile = pl.BlockSpec((TILE_TOKENS, width), lambda t, ids, cnt: (t, 0))
    partial = jax.ShapeDtypeStruct((rows, width), jnp.float32)
    acc, tot = pl.pallas_call(
        functools.partial(attention_kernel, local_heads, per_patch, False),
        out_shape=(partial, partial),
        grid_spec=pltpu.PrefetchScalarGridSpec(
            num_scalar_prefetch=2,
            grid=(tiles,),
            in_specs=[resident],
            out_specs=(tile, tile),
            scratch_shapes=[pltpu.SMEM((KEY_SLOTS,), jnp.int32)],
        ),
    )(local_ids, tile_count, fresh)
    hbm = pl.BlockSpec(memory_space=pl.ANY)
    return pl.pallas_call(
        functools.partial(attention_kernel, local_heads, per_patch, True),
        out_shape=jax.ShapeDtypeStruct((rows, width), jnp.bfloat16),
        grid_spec=pltpu.PrefetchScalarGridSpec(
            num_scalar_prefetch=2,
            grid=(tiles,),
            in_specs=[resident, hbm, resident, tile, tile],
            out_specs=tile,
            scratch_shapes=[
                pltpu.VMEM((2 * rows, before.shape[1]), before.dtype),
                pltpu.SemaphoreType.DMA((2,)),
                pltpu.SMEM((KEY_SLOTS,), jnp.int32),
                pltpu.VMEM((TILE_TOKENS, HEAD_DIM), jnp.float32),
                pltpu.VMEM((TILE_TOKENS, HEAD_DIM), jnp.float32),
            ],
        ),
        compiler_params=pltpu.CompilerParams(dimension_semantics=("arbitrary",)),
    )(local_ids, tile_count, fresh, before, after, acc, tot)


def regroup_kernel(width, *refs):
    *in_refs, o_ref = refs
    seq_count = o_ref.shape[0]
    for d in range(seq_count):
        for a, ref in enumerate(in_refs):
            o_ref[d, :, a * width:(a + 1) * width] = ref[:, d * width:(d + 1) * width]


def regroup(arrays, seq_count, width):
    rows = arrays[0].shape[0]
    return pl.pallas_call(
        functools.partial(regroup_kernel, width),
        out_shape=jax.ShapeDtypeStruct((seq_count, rows, len(arrays) * width), arrays[0].dtype),
    )(*arrays)


def on_device(query, fresh_key, fresh_value, stale_key, stale_value, key_tiles, tile_count):
    seq_count = lax.axis_size("seq")
    local_heads = NUM_HEADS // seq_count
    width = local_heads * HEAD_DIM
    per_patch = TILES_H * TILES_W
    rows = query.shape[0]
    patch_rows = rows * seq_count

    def interleaved(arrays):
        parts = [a.reshape(rows, seq_count, width) for a in arrays]
        joined = jnp.concatenate(parts, axis=2).transpose(1, 0, 2)
        moved = lax.all_to_all(joined, "seq", split_axis=0, concat_axis=0, tiled=True)
        return moved.reshape(patch_rows, len(arrays) * width)

    joined = regroup([stale_key, stale_value], seq_count, width)
    stale = lax.all_to_all(joined, "seq", split_axis=0, concat_axis=0, tiled=True)
    stale = stale.reshape(patch_rows, 2 * width)
    framed = with_halo(stale, (("patch", 0),), patch_rows)
    before = framed[:patch_rows]
    after = framed[2 * patch_rows :]
    fresh = interleaved([query, fresh_key, fresh_value])
    first_tile = (lax.axis_index("patch") - 1) * per_patch
    local_ids = (key_tiles - first_tile).astype(jnp.int32)
    merged = tile_attention(
        fresh, before, after, local_ids, tile_count.astype(jnp.int32), local_heads, per_patch
    )
    return lax.all_to_all(merged, "seq", split_axis=0, concat_axis=1, tiled=True)


def solution(mesh):
    return jax.shard_map(
        on_device,
        mesh=mesh,
        in_specs=(
            P(("cfg", "patch", "seq"), None),
            P(("cfg", "patch", "seq"), None),
            P(("cfg", "patch", "seq"), None),
            P(("cfg", "patch", "seq"), None),
            P(("cfg", "patch", "seq"), None),
            P("patch", None),
            P("patch"),
        ),
        out_specs=P(("cfg", "patch", "seq"), None),
        check_vma=False,
    )
```
